32 devices in a mesh: dp: 8 (over z, core), expert: 4 (over y, x).
Axes of the slice: x: 2, y: 2, z: 4, core: 2. Of those that a mesh axis runs over, the one named last changes fastest.
Arguments:
- activations: bfloat16 [2048, 8, 768], P(('dp', 'expert')), may hold values from -6 to 6
- out_grad: bfloat16 [2048, 2048], P(('dp', 'expert')), may hold values from -0.796875 to 0.796875
- gate_weights: float32 [2048, 8], P(('dp', 'expert')), may hold values from 0.02 to 0.3
- routes: int32 [2048, 8], P(('dp', 'expert')), may hold values from 0 to 15, all different within a row; in each aligned block of 64 rows (0 to 63, 64 to 127, ...) at most 64 rows name the same one
- momentum: float32 [32768, 768], P(('expert', 'dp')), may hold values from -4 to 4
Outputs:
- update: bfloat16 [32768, 768], P(('expert', 'dp'))
- new_momentum: float32 [32768, 768], P(('expert', 'dp'))
The draws below stay inside these ranges and needn't reach their ends.
Inputs may be any that keep to these rules, and one draw needn't show every extreme that they name: `routes`: each row names 8 different experts. Among the 64 rows of one device no expert is named by more than 64 rows, and in every draw some expert is named by exactly 64 rows of some device.
All inputs are finite; a program needn't handle non-finite values.
Results may differ from the reference program's by a relative error of at most 0.029.
Values may be sent and summed in bfloat16 or wider, within the bound.
No kernel may reach another device: no remote copies, remote signals or barrier semaphores. Data moves between devices by JAX's collectives and lax.ppermute only.
A program may use at most 128 MiB of HBM per device.

```python
import math
import jax
import jax.numpy as jnp
import numpy as np
from jax import lax

D = 2048
FF = 768
TOPK = 8
NS_ITERS = 2
TOK_DEV = 64
EXPERTS = 16
CAP = 64
TOKENS = 2048
N_DP = 8
N_EXPERT = 4


def block_levels(own_key, shape, shards, smallest, top_value):
    def one(axis_at, blocks):
        steps = jax.random.uniform(jax.random.fold_in(jax.random.fold_in(own_key, 6), axis_at), (blocks,), jnp.float32, smallest / len(shards), top_value / len(shards))
        return jnp.repeat(jnp.exp(steps), shape[axis_at] // blocks).reshape((-1,) + (1,) * (len(shape) - axis_at - 1))

    level = one(*shards[0])
    for cut in shards[1:]:
        level = level * one(*cut)
    return level


def routed_block(key, own, number, rows, amount, top, most, slope):
    ranking = jax.random.permutation(key, amount)
    crowded, common = shares(amount, rows * top, most, slope, True), shares(amount, rows * top, most, slope, False)
    places = jnp.arange(amount)

    def named(sizes, turn):
        used = int((sizes > 0).sum())
        fixed = max(1, used // 4)
        passed = fixed + (places - fixed + turn * (used - fixed)) % max(1, amount - fixed)
        return jnp.zeros((amount,), jnp.int32).at[ranking[jnp.where(places < fixed, places, passed)]].set(jnp.asarray(sizes, jnp.int32))

    sizes = jnp.where(number % 4 == 0, named(crowded, number // 4), named(common, number - number // 4 - 1))
    mixed = jax.random.permutation(jax.random.fold_in(own, 3), amount)
    giver, taker = mixed[0:amount // 2 * 2:2], mixed[1:amount // 2 * 2:2]
    margin = jnp.minimum(sizes[giver] - 1, most - sizes[taker]) // 2
    margin = jnp.where((giver == ranking[0]) | (taker == ranking[0]) | (sizes[taker] == 0), 0, jnp.maximum(margin, 0))
    passed = jax.random.randint(jax.random.fold_in(own, 4), (amount // 2,), 0, 1 << 20) % (margin + 1)
    sizes = sizes.at[giver].add(-passed).at[taker].add(passed)
    labels = jnp.searchsorted(jnp.cumsum(sizes), jnp.arange(rows * top), side="right").astype(jnp.int32)
    table = labels.reshape(top, rows).T
    table = table[jax.random.permutation(jax.random.fold_in(own, 1), rows)]
    turn = jax.random.randint(jax.random.fold_in(own, 2), (rows, 1), 0, top)
    return jnp.take_along_axis(table, (jnp.arange(top)[None, :] + turn) % top, axis=1)


def shares(amount, total, bound, slope, full):
    weights = [(1 << 20) // math.isqrt(standing ** slope) + 1 for standing in range(1, amount + 1)]
    largest = bound if full else min(bound, max(-(-total // amount), total * weights[0] // sum(weights)))
    least = 1 if total - largest >= amount - 1 else 0
    given, spare = [largest] + [least] * (amount - 1), total - largest - least * (amount - 1)
    while spare > 0:
        free = [i for i in range(1, amount) if given[i] < largest] or [i for i in range(1, amount) if given[i] < bound]
        mass, budget = sum([weights[i] for i in free]), spare
        for i in free:
            extra = min(bound - given[i], max(1, budget * weights[i] // mass), spare)
            given[i] = given[i] + extra
            spare = spare - extra
    return np.array(given)


def normal_values(key, dims, spread, reach, split=(), kind=jnp.bfloat16):
    values = spread * jax.random.normal(key, dims, jnp.float32)
    if split:
        values = values * block_levels(key, dims, split, -0.22, 0.18)
    return jnp.clip(values, -reach, reach).astype(kind)


def setup_inputs(seed: int = 0) -> dict:
    streams_of = jax.random.split(jax.random.key(seed), 6)
    activations = normal_values(streams_of[0], (TOKENS, TOPK, FF), 1.0, 6.0, ((0, 32),))
    out_grad = normal_values(streams_of[1], (TOKENS, D), 0.1, 0.796875, ((0, 32),))
    gate_weights = jnp.clip(jnp.exp(math.log(0.3) - 2.7080503 * jax.random.uniform(streams_of[2], (TOKENS, TOPK), jnp.float32) ** block_levels(streams_of[2], (TOKENS, TOPK), ((0, 32),), -0.2, 0.2)), 0.02, 0.3)
    routes_keys = jax.random.split(jax.random.fold_in(streams_of[3], 1), TOKENS // TOK_DEV)
    routes_turns = jax.random.permutation(jax.random.fold_in(streams_of[3], 3), TOKENS // TOK_DEV)
    routes = jax.vmap(lambda own, number: routed_block(jax.random.fold_in(streams_of[3], 2), own, number, TOK_DEV, EXPERTS, TOPK, CAP, 2))(routes_keys, routes_turns).reshape((TOKENS, TOPK))
    momentum = normal_values(streams_of[4], (EXPERTS * D, FF), 0.5, 4.0, ((0, 32),), jnp.float32)
    return {"activations": activations, "out_grad": out_grad, "gate_weights": gate_weights, "routes": routes, "momentum": momentum}


MOMENT = 0.95
COEFF_A = 3.4445
COEFF_B = -4.775
COEFF_C = 2.0315
EPSILON = 1e-07

def slot_table(routing, expert_total, capacity):
    tokens_here = routing.shape[0]
    slots_token = routing.shape[1]
    numbers = jnp.arange(expert_total, dtype=jnp.int32)
    matched = (routing[:, :, None] == numbers[None, None, :]).astype(jnp.int32)
    named_by = lax.optimization_barrier(jnp.sum(matched, axis=1))
    position = lax.optimization_barrier(jnp.sum(matched * jnp.arange(slots_token, dtype=jnp.int32)[None, :, None], axis=1))
    earlier = jnp.cumsum(named_by, axis=0) - named_by
    places = jnp.arange(capacity, dtype=jnp.int32)
    picked = ((named_by[:, :, None] == 1) & (earlier[:, :, None] == places[None, None, :])).astype(jnp.int32)
    pair_index = jnp.arange(tokens_here, dtype=jnp.int32)[:, None] * slots_token + position
    source = lax.optimization_barrier(jnp.sum(picked * pair_index[:, :, None], axis=0)).astype(jnp.int32)
    filled = lax.optimization_barrier(jnp.sum(picked, axis=0)) > 0
    return (source, filled)

def pack_slots(hidden_block, grad_block, gate_block, source, filled, slots_token):
    hidden_rows = hidden_block.reshape(-1, hidden_block.shape[-1])
    picked_rows = jnp.where(filled[..., None], jnp.take(hidden_rows, source, axis=0), jnp.zeros((), hidden_rows.dtype))
    scales = jnp.where(filled, jnp.take(gate_block.reshape(-1), source), jnp.zeros((), jnp.float32))
    grad_rows = jnp.take(grad_block, source // slots_token, axis=0).astype(jnp.float32)
    weighted = (scales[..., None] * grad_rows).astype(jnp.bfloat16)
    return (picked_rows, weighted)

def device_slots(hidden_block, grad_block, gate_block, route_block):
    source, filled = slot_table(route_block, EXPERTS, CAP)
    return pack_slots(hidden_block, grad_block, gate_block, source, filled, TOPK)

def newton_update(scaled, gram):
    square = jnp.dot(gram, gram, preferred_element_type=jnp.float32)
    poly = (COEFF_B * gram.astype(jnp.float32) + COEFF_C * square).astype(jnp.bfloat16)
    product = jnp.dot(scaled, poly, preferred_element_type=jnp.float32)
    return (COEFF_A * scaled.astype(jnp.float32) + product).astype(jnp.bfloat16)

def orthogonal(ahead):
    norm_value = jnp.sqrt(jnp.sum(ahead * ahead))
    scaled = (ahead / (norm_value + EPSILON)).astype(jnp.bfloat16)
    for turn_index in range(NS_ITERS):
        gram = lax.dot_general(scaled, scaled, (((0,), (0,)), ((), ())), preferred_element_type=jnp.float32).astype(jnp.bfloat16)
        scaled = newton_update(scaled, gram)
    return (math.sqrt(D) * scaled.astype(jnp.float32)).astype(jnp.bfloat16)

def reference(activations, out_grad, gate_weights, routes, momentum):
    hidden = activations.reshape(N_DP, N_EXPERT, TOK_DEV, TOPK, FF)
    grads = out_grad.reshape(N_DP, N_EXPERT, TOK_DEV, D)
    gates = gate_weights.reshape(N_DP, N_EXPERT, TOK_DEV, TOPK)
    routing = routes.reshape(N_DP, N_EXPERT, TOK_DEV, TOPK)

    def add_rank(running, inputs):
        hidden_rank, grad_rank, gate_rank, route_rank = inputs
        slot_rows, slot_weighted = jax.vmap(device_slots)(hidden_rank, grad_rank, gate_rank, route_rank)
        partial_value = jnp.einsum('qecd,qecf->edf', slot_weighted.astype(jnp.float32), slot_rows.astype(jnp.float32), precision=lax.Precision.HIGHEST)
        rounded = lax.optimization_barrier(partial_value.astype(jnp.bfloat16))
        return (running + rounded.astype(jnp.float32), None)
    start_sum = jnp.zeros((EXPERTS, D, FF), jnp.float32)
    gradient, unused = lax.scan(add_rank, start_sum, (hidden, grads, gates, routing))
    previous = momentum.reshape(EXPERTS, D, FF)
    new_momentum = MOMENT * previous + gradient
    ahead = gradient + MOMENT * new_momentum
    update = lax.map(orthogonal, ahead)
    return (update.reshape(EXPERTS * D, FF), new_momentum.reshape(EXPERTS * D, FF))
```

```python
import math

import jax
import jax.numpy as jnp
import numpy as np
from jax import lax
from jax.sharding import Mesh
from jax.sharding import PartitionSpec as P

EXP_DEV = 4
NS_ITERS = 2


MOMENT = 0.95
COEFF_A = 3.4445
COEFF_B = -4.775
COEFF_C = 2.0315
EPSILON = 1e-07


def newton_update(scaled, gram):
    square = jnp.dot(gram, gram, preferred_element_type=jnp.float32)
    poly = (COEFF_B * gram.astype(jnp.float32) + COEFF_C * square).astype(jnp.bfloat16)
    product = jnp.dot(scaled, poly, preferred_element_type=jnp.float32)
    return (COEFF_A * scaled.astype(jnp.float32) + product).astype(jnp.bfloat16)


def gram_of(scaled):
    return lax.dot_general(
        scaled, scaled, (((0,), (0,)), ((), ())), preferred_element_type=jnp.float32
    )


def body(activations, out_grad, gate_weights, routes, momentum):
    expert_count = lax.axis_size("expert")
    zlo_count = lax.axis_size("zlo")
    zhi_count = lax.axis_size("zhi")
    z_count = zhi_count * zlo_count
    tokens_here, slots_token, hidden_width = activations.shape
    model_width = out_grad.shape[1]
    own_rows = momentum.shape[0]
    expert_total = EXP_DEV * expert_count
    half_blocks = model_width // (2 * own_rows)

    numbers = jnp.arange(expert_total, dtype=jnp.int32)
    matched = routes[:, :, None] == numbers[None, None, :]
    flat_hidden = activations.reshape(tokens_here * slots_token, hidden_width)
    eye = (
        jnp.arange(tokens_here, dtype=jnp.int32)[:, None, None]
        == jnp.arange(tokens_here, dtype=jnp.int32)[None, :, None]
    )
    selector = (matched.transpose(2, 0, 1)[:, :, None, :] & eye[None]).astype(jnp.bfloat16)
    selector = selector.reshape(expert_total * tokens_here, tokens_here * slots_token)
    chosen = jnp.dot(selector, flat_hidden, preferred_element_type=jnp.float32)
    scale = jnp.sum(jnp.where(matched, gate_weights[:, :, None], 0.0), axis=1)
    scale = scale.T.reshape(expert_total * tokens_here, 1)
    scaled_hidden = (scale * chosen).astype(jnp.bfloat16)
    scaled_hidden = scaled_hidden.reshape(expert_count, EXP_DEV, tokens_here, hidden_width)
    scaled_hidden = scaled_hidden.transpose(1, 0, 2, 3)
    got_hidden = lax.all_to_all(scaled_hidden, "expert", split_axis=1, concat_axis=1, tiled=True)
    got_hidden = lax.all_gather(got_hidden, "core", axis=1, tiled=False)
    got_hidden = got_hidden.reshape(EXP_DEV, 2 * expert_count * tokens_here, hidden_width)

    grad_parts = out_grad.reshape(tokens_here, half_blocks, 2, own_rows)
    grad_mine = lax.all_to_all(grad_parts, "core", split_axis=2, concat_axis=2, tiled=True)
    grad_mine = grad_mine.transpose(2, 0, 1, 3).reshape(2, tokens_here, half_blocks * own_rows)
    grad_all = lax.all_gather(grad_mine, "expert", axis=1, tiled=False)
    grad_all = grad_all.reshape(2 * expert_count * tokens_here, half_blocks * own_rows)

    partial = jnp.einsum(
        "td,etf->edf", grad_all, got_hidden, preferred_element_type=jnp.float32
    ).astype(jnp.bfloat16)
    partial = partial.reshape(z_count * own_rows, hidden_width)
    gradient = lax.psum_scatter(
        partial, ("zhi", "zlo"), scatter_dimension=0, tiled=True
    ).astype(jnp.float32)

    new_momentum = MOMENT * momentum + gradient
    ahead = gradient + MOMENT * new_momentum
    group = ("zlo", "core")
    member = lax.axis_index("zlo") * 2 + lax.axis_index("core")
    square_sum = lax.psum(jnp.sum(ahead * ahead), group)
    norm_value = jnp.sqrt(square_sum)
    scaled = (ahead / (norm_value + EPSILON)).astype(jnp.bfloat16)
    scaled_whole = lax.all_gather(scaled, group, axis=0, tiled=True)
    for turn_index in range(NS_ITERS):
        gram = gram_of(scaled_whole).astype(jnp.bfloat16)
        scaled_whole = newton_update(scaled_whole, gram)
    scaled = lax.dynamic_slice_in_dim(scaled_whole, member * own_rows, own_rows, 0)
    update = (math.sqrt(model_width) * scaled.astype(jnp.float32)).astype(jnp.bfloat16)
    return (update, new_momentum)


def solution(mesh):
    dp_count = mesh.shape["dp"]
    expert_count = mesh.shape["expert"]
    group_size = dp_count // EXP_DEV
    zlo = group_size // 2
    zhi = dp_count // 2 // zlo
    devices = np.asarray(mesh.devices).reshape(zhi, zlo, 2, expert_count)
    fine = Mesh(devices, ("zhi", "zlo", "core", "expert"))
    rows = ("zhi", "zlo", "core", "expert")
    cols = ("expert", "zhi", "zlo", "core")
    in_specs = (
        P(rows, None, None),
        P(rows, None),
        P(rows, None),
        P(rows, None),
        P(cols, None),
    )
    out_specs = (P(cols, None), P(cols, None))
    return jax.shard_map(body, mesh=fine, in_specs=in_specs, out_specs=out_specs, check_vma=False)
```

```python
import math

import jax
import jax.numpy as jnp
import numpy as np
from jax import lax
from jax.sharding import Mesh
from jax.sharding import PartitionSpec as P

EXP_DEV = 4
NS_ITERS = 2


MOMENT = 0.95
COEFF_A = 3.4445
COEFF_B = -4.775
COEFF_C = 2.0315
EPSILON = 1e-07


def newton_update(scaled, gram):
    square = jnp.dot(gram, gram, preferred_element_type=jnp.float32)
    poly = (COEFF_B * gram.astype(jnp.float32) + COEFF_C * square).astype(jnp.bfloat16)
    product = jnp.dot(scaled, poly, preferred_element_type=jnp.float32)
    return (COEFF_A * scaled.astype(jnp.float32) + product).astype(jnp.bfloat16)


def gram_of(scaled):
    return lax.dot_general(
        scaled, scaled, (((0,), (0,)), ((), ())), preferred_element_type=jnp.float32
    )


def body(activations, out_grad, gate_weights, routes, momentum):
    expert_count = lax.axis_size("expert")
    zlo_count = lax.axis_size("zlo")
    zhi_count = lax.axis_size("zhi")
    z_count = zhi_count * zlo_count
    tokens_here, slots_token, hidden_width = activations.shape
    model_width = out_grad.shape[1]
    own_rows = momentum.shape[0]
    expert_total = EXP_DEV * expert_count
    group_size = zlo_count * 2
    group = ("zlo", "core")

    numbers = jnp.arange(expert_total, dtype=jnp.int32)
    matched = routes[:, :, None] == numbers[None, None, :]
    flat_hidden = activations.reshape(tokens_here * slots_token, hidden_width)
    eye = (
        jnp.arange(tokens_here, dtype=jnp.int32)[:, None, None]
        == jnp.arange(tokens_here, dtype=jnp.int32)[None, :, None]
    )
    selector = (matched.transpose(2, 0, 1)[:, :, None, :] & eye[None]).astype(jnp.bfloat16)
    selector = selector.reshape(expert_total * tokens_here, tokens_here * slots_token)
    chosen = jnp.dot(selector, flat_hidden, preferred_element_type=jnp.float32)
    scale = jnp.sum(jnp.where(matched, gate_weights[:, :, None], 0.0), axis=1)
    scale = scale.T.reshape(expert_total * tokens_here, 1)
    scaled_hidden = (scale * chosen).astype(jnp.bfloat16)
    scaled_hidden = scaled_hidden.reshape(expert_count, EXP_DEV, tokens_here, hidden_width)
    scaled_hidden = scaled_hidden.transpose(1, 0, 2, 3).reshape(expert_total, tokens_here, hidden_width)
    got_hidden = lax.all_to_all(
        scaled_hidden, ("zhi", "expert"), split_axis=0, concat_axis=0, tiled=True
    )
    got_hidden = lax.all_gather(got_hidden, group, axis=1, tiled=False)
    got_hidden = got_hidden.reshape(-1, hidden_width)

    grad_parts = out_grad.reshape(tokens_here, group_size, own_rows)
    grad_mine = lax.all_to_all(grad_parts, group, split_axis=1, concat_axis=1, tiled=True)
    grad_mine = grad_mine.transpose(1, 0, 2)
    grad_all = lax.all_gather(grad_mine, ("zhi", "expert"), axis=0, tiled=False)
    grad_all = grad_all.reshape(-1, own_rows)

    gradient = lax.dot_general(
        grad_all, got_hidden, (((0,), (0,)), ((), ())), preferred_element_type=jnp.float32
    )

    new_momentum = MOMENT * momentum + gradient
    ahead = gradient + MOMENT * new_momentum
    member = lax.axis_index("zlo") * 2 + lax.axis_index("core")
    square_sum = lax.psum(jnp.sum(ahead * ahead), group)
    norm_value = jnp.sqrt(square_sum)
    scaled = (ahead / (norm_value + EPSILON)).astype(jnp.bfloat16)
    scaled_whole = lax.all_gather(scaled, group, axis=0, tiled=True)
    for turn_index in range(NS_ITERS):
        gram = gram_of(scaled_whole).astype(jnp.bfloat16)
        scaled_whole = newton_update(scaled_whole, gram)
    scaled = lax.dynamic_slice_in_dim(scaled_whole, member * own_rows, own_rows, 0)
    update = (math.sqrt(model_width) * scaled.astype(jnp.float32)).astype(jnp.bfloat16)
    return (update, new_momentum)


def solution(mesh):
    dp_count = mesh.shape["dp"]
    expert_count = mesh.shape["expert"]
    group_size = dp_count // EXP_DEV
    zlo = group_size // 2
    zhi = dp_count // 2 // zlo
    devices = np.asarray(mesh.devices).reshape(zhi, zlo, 2, expert_count)
    fine = Mesh(devices, ("zhi", "zlo", "core", "expert"))
    rows = ("zhi", "zlo", "core", "expert")
    cols = ("expert", "zhi", "zlo", "core")
    in_specs = (
        P(rows, None, None),
        P(rows, None),
        P(rows, None),
        P(rows, None),
        P(cols, None),
    )
    out_specs = (P(cols, None), P(cols, None))
    return jax.shard_map(body, mesh=fine, in_specs=in_specs, out_specs=out_specs, check_vma=False)
```

```python
import math

import jax
import jax.numpy as jnp
import numpy as np
from jax import lax
from jax.sharding import Mesh
from jax.sharding import PartitionSpec as P

EXP_DEV = 4
NS_ITERS = 2


MOMENT = 0.95
COEFF_A = 3.4445
COEFF_B = -4.775
COEFF_C = 2.0315
EPSILON = 1e-07


def newton_update(scaled, gram):
    square = jnp.dot(gram, gram, preferred_element_type=jnp.float32)
    poly = (COEFF_B * gram.astype(jnp.float32) + COEFF_C * square).astype(jnp.bfloat16)
    product = jnp.dot(scaled, poly, preferred_element_type=jnp.float32)
    return (COEFF_A * scaled.astype(jnp.float32) + product).astype(jnp.bfloat16)


def gram_of(scaled):
    return lax.dot_general(
        scaled, scaled, (((0,), (0,)), ((), ())), preferred_element_type=jnp.float32
    )


def group_gather(block, axes, count):
    member = lax.axis_index(axes)
    parts = [block]
    for shift in range(1, count):
        route = [(source, (source + shift) % count) for source in range(count)]
        parts.append(lax.ppermute(block, axes, route))
    stacked = jnp.stack(parts)
    order = (member - jnp.arange(count, dtype=jnp.int32)) % count
    return jnp.take(stacked, order, axis=0)


def body(activations, out_grad, gate_weights, routes, momentum):
    expert_count = lax.axis_size("expert")
    zlo_count = lax.axis_size("zlo")
    zhi_count = lax.axis_size("zhi")
    z_count = zhi_count * zlo_count
    tokens_here, slots_token, hidden_width = activations.shape
    model_width = out_grad.shape[1]
    own_rows = momentum.shape[0]
    expert_total = EXP_DEV * expert_count
    group_size = zlo_count * 2
    group = ("zlo", "core")

    grad_parts = out_grad.reshape(tokens_here, group_size, own_rows)
    grad_mine = lax.all_to_all(grad_parts, group, split_axis=1, concat_axis=1, tiled=True)
    grad_mine = grad_mine.transpose(1, 0, 2)
    grad_mine, activations = lax.optimization_barrier((grad_mine, activations))
    grad_all = lax.all_gather(grad_mine, ("zhi", "expert"), axis=0, tiled=False)
    grad_all = grad_all.reshape(-1, own_rows)

    numbers = jnp.arange(expert_total, dtype=jnp.int32)
    matched = routes[:, :, None] == numbers[None, None, :]
    flat_hidden = activations.reshape(tokens_here * slots_token, hidden_width)
    eye = (
        jnp.arange(tokens_here, dtype=jnp.int32)[:, None, None]
        == jnp.arange(tokens_here, dtype=jnp.int32)[None, :, None]
    )
    selector = (matched.transpose(2, 0, 1)[:, :, None, :] & eye[None]).astype(jnp.bfloat16)
    selector = selector.reshape(expert_total * tokens_here, tokens_here * slots_token)
    chosen = jnp.dot(selector, flat_hidden, preferred_element_type=jnp.float32)
    scale = jnp.sum(jnp.where(matched, gate_weights[:, :, None], 0.0), axis=1)
    scale = scale.T.reshape(expert_total * tokens_here, 1)
    scaled_hidden = (scale * chosen).astype(jnp.bfloat16)
    scaled_hidden = scaled_hidden.reshape(expert_count, EXP_DEV, tokens_here, hidden_width)
    scaled_hidden = scaled_hidden.transpose(1, 0, 2, 3).reshape(expert_total, tokens_here, hidden_width)
    got_hidden = lax.all_to_all(
        scaled_hidden, ("zhi", "expert"), split_axis=0, concat_axis=0, tiled=True
    )
    got_hidden = group_gather(got_hidden, group, group_size)
    got_hidden = got_hidden.transpose(1, 0, 2, 3).reshape(-1, hidden_width)

    gradient = lax.dot_general(
        grad_all, got_hidden, (((0,), (0,)), ((), ())), preferred_element_type=jnp.float32
    )

    new_momentum = MOMENT * momentum + gradient
    ahead = gradient + MOMENT * new_momentum
    member = lax.axis_index("zlo") * 2 + lax.axis_index("core")
    square_sum = lax.psum(jnp.sum(ahead * ahead), group)
    norm_value = jnp.sqrt(square_sum)
    scaled = (ahead / (norm_value + EPSILON)).astype(jnp.bfloat16)
    scaled_whole = lax.all_gather(scaled, group, axis=0, tiled=True)
    for turn_index in range(NS_ITERS):
        gram = gram_of(scaled_whole).astype(jnp.bfloat16)
        scaled_whole = newton_update(scaled_whole, gram)
    scaled = lax.dynamic_slice_in_dim(scaled_whole, member * own_rows, own_rows, 0)
    update = (math.sqrt(model_width) * scaled.astype(jnp.float32)).astype(jnp.bfloat16)
    return (update, new_momentum)


def solution(mesh):
    dp_count = mesh.shape["dp"]
    expert_count = mesh.shape["expert"]
    group_size = dp_count // EXP_DEV
    zlo = group_size // 2
    zhi = dp_count // 2 // zlo
    devices = np.asarray(mesh.devices).reshape(zhi, zlo, 2, expert_count)
    fine = Mesh(devices, ("zhi", "zlo", "core", "expert"))
    rows = ("zhi", "zlo", "core", "expert")
    cols = ("expert", "zhi", "zlo", "core")
    in_specs = (
        P(rows, None, None),
        P(rows, None),
        P(rows, None),
        P(rows, None),
        P(cols, None),
    )
    out_specs = (P(cols, None), P(cols, None))
    return jax.shard_map(body, mesh=fine, in_specs=in_specs, out_specs=out_specs, check_vma=False)
```

```python
import math

import jax
import jax.numpy as jnp
import numpy as np
from jax import lax
from jax.sharding import Mesh
from jax.sharding import PartitionSpec as P

EXP_DEV = 4
NS_ITERS = 2


MOMENT = 0.95
COEFF_A = 3.4445
COEFF_B = -4.775
COEFF_C = 2.0315
EPSILON = 1e-07


def newton_update(scaled, gram):
    square = jnp.dot(gram, gram, preferred_element_type=jnp.float32)
    poly = (COEFF_B * gram.astype(jnp.float32) + COEFF_C * square).astype(jnp.bfloat16)
    product = jnp.dot(scaled, poly, preferred_element_type=jnp.float32)
    return (COEFF_A * scaled.astype(jnp.float32) + product).astype(jnp.bfloat16)


def gram_of(scaled):
    return lax.dot_general(
        scaled, scaled, (((0,), (0,)), ((), ())), preferred_element_type=jnp.float32
    )


def group_gather(block, axes, count):
    member = lax.axis_index(axes)
    parts = [block]
    for shift in range(1, count):
        route = [(source, (source + shift) % count) for source in range(count)]
        parts.append(lax.ppermute(block, axes, route))
    stacked = jnp.stack(parts)
    order = (member - jnp.arange(count, dtype=jnp.int32)) % count
    return jnp.take(stacked, order, axis=0)


def group_exchange(parts, axes, count):
    member = lax.axis_index(axes)
    got = [lax.dynamic_index_in_dim(parts, member, 0, keepdims=False)]
    for shift in range(1, count):
        route = [(source, (source + shift) % count) for source in range(count)]
        send = lax.dynamic_index_in_dim(parts, (member + shift) % count, 0, keepdims=False)
        got.append(lax.ppermute(send, axes, route))
    stacked = jnp.stack(got)
    order = (member - jnp.arange(count, dtype=jnp.int32)) % count
    return jnp.take(stacked, order, axis=0)


def group_sum(value, axes, count):
    return jnp.sum(group_gather(value, axes, count), axis=0)


def body(activations, out_grad, gate_weights, routes, momentum):
    expert_count = lax.axis_size("expert")
    zlo_count = lax.axis_size("zlo")
    zhi_count = lax.axis_size("zhi")
    z_count = zhi_count * zlo_count
    tokens_here, slots_token, hidden_width = activations.shape
    model_width = out_grad.shape[1]
    own_rows = momentum.shape[0]
    expert_total = EXP_DEV * expert_count
    group_size = zlo_count * 2
    group = ("zlo", "core")

    grad_parts = out_grad.reshape(tokens_here, group_size, own_rows).transpose(1, 0, 2)
    grad_mine = group_exchange(grad_parts, group, group_size)
    grad_mine, activations = lax.optimization_barrier((grad_mine, activations))
    grad_all = lax.all_gather(grad_mine, ("zhi", "expert"), axis=0, tiled=False)
    grad_all = grad_all.reshape(-1, own_rows)

    numbers = jnp.arange(expert_total, dtype=jnp.int32)
    matched = routes[:, :, None] == numbers[None, None, :]
    flat_hidden = activations.reshape(tokens_here * slots_token, hidden_width)
    eye = (
        jnp.arange(tokens_here, dtype=jnp.int32)[:, None, None]
        == jnp.arange(tokens_here, dtype=jnp.int32)[None, :, None]
    )
    selector = (matched.transpose(2, 0, 1)[:, :, None, :] & eye[None]).astype(jnp.bfloat16)
    selector = selector.reshape(expert_total * tokens_here, tokens_here * slots_token)
    chosen = jnp.dot(selector, flat_hidden, preferred_element_type=jnp.float32)
    scale = jnp.sum(jnp.where(matched, gate_weights[:, :, None], 0.0), axis=1)
    scale = scale.T.reshape(expert_total * tokens_here, 1)
    scaled_hidden = (scale * chosen).astype(jnp.bfloat16)
    scaled_hidden = scaled_hidden.reshape(expert_count, EXP_DEV, tokens_here, hidden_width)
    scaled_hidden = scaled_hidden.transpose(1, 0, 2, 3).reshape(expert_total, tokens_here, hidden_width)
    got_hidden = lax.all_to_all(
        scaled_hidden, ("zhi", "expert"), split_axis=0, concat_axis=0, tiled=True
    )
    got_hidden = group_gather(got_hidden, group, group_size)
    got_hidden = got_hidden.transpose(1, 0, 2, 3).reshape(-1, hidden_width)

    gradient = lax.dot_general(
        grad_all, got_hidden, (((0,), (0,)), ((), ())), preferred_element_type=jnp.float32
    )

    new_momentum = MOMENT * momentum + gradient
    ahead = gradient + MOMENT * new_momentum
    square_sum = group_sum(jnp.sum(ahead * ahead), group, group_size)
    norm_value = jnp.sqrt(square_sum)
    scaled = (ahead / (norm_value + EPSILON)).astype(jnp.bfloat16)
    for turn_index in range(NS_ITERS):
        gram = group_sum(gram_of(scaled), group, group_size).astype(jnp.bfloat16)
        scaled = newton_update(scaled, gram)
    update = (math.sqrt(model_width) * scaled.astype(jnp.float32)).astype(jnp.bfloat16)
    return (update, new_momentum)


def solution(mesh):
    dp_count = mesh.shape["dp"]
    expert_count = mesh.shape["expert"]
    group_size = dp_count // EXP_DEV
    zlo = group_size // 2
    zhi = dp_count // 2 // zlo
    devices = np.asarray(mesh.devices).reshape(zhi, zlo, 2, expert_count)
    fine = Mesh(devices, ("zhi", "zlo", "core", "expert"))
    rows = ("zhi", "zlo", "core", "expert")
    cols = ("expert", "zhi", "zlo", "core")
    in_specs = (
        P(rows, None, None),
        P(rows, None),
        P(rows, None),
        P(rows, None),
        P(cols, None),
    )
    out_specs = (P(cols, None), P(cols, None))
    return jax.shard_map(body, mesh=fine, in_specs=in_specs, out_specs=out_specs, check_vma=False)
```

```python
import math

import jax
import jax.numpy as jnp
import numpy as np
from jax import lax
from jax.sharding import Mesh
from jax.sharding import PartitionSpec as P

EXP_DEV = 4
NS_ITERS = 2


MOMENT = 0.95
COEFF_A = 3.4445
COEFF_B = -4.775
COEFF_C = 2.0315
EPSILON = 1e-07


def newton_update(scaled, gram):
    square = jnp.dot(gram, gram, preferred_element_type=jnp.float32)
    poly = (COEFF_B * gram.astype(jnp.float32) + COEFF_C * square).astype(jnp.bfloat16)
    product = jnp.dot(scaled, poly, preferred_element_type=jnp.float32)
    return (COEFF_A * scaled.astype(jnp.float32) + product).astype(jnp.bfloat16)


def gram_of(scaled):
    return lax.dot_general(
        scaled, scaled, (((0,), (0,)), ((), ())), preferred_element_type=jnp.float32
    )


def group_gather(block, axes, count):
    parts = [block]
    for shift in range(1, count):
        route = [(source, (source + shift) % count) for source in range(count)]
        parts.append(lax.ppermute(block, axes, route))
    return jnp.stack(parts)


def group_exchange(parts, axes, count):
    member = lax.axis_index(axes)
    got = [lax.dynamic_index_in_dim(parts, member, 0, keepdims=False)]
    for shift in range(1, count):
        route = [(source, (source + shift) % count) for source in range(count)]
        send = lax.dynamic_index_in_dim(parts, (member + shift) % count, 0, keepdims=False)
        got.append(lax.ppermute(send, axes, route))
    return jnp.stack(got)


def group_sum(value, axes, count):
    total = value
    for shift in range(1, count):
        route = [(source, (source + shift) % count) for source in range(count)]
        total = total + lax.ppermute(value, axes, route)
    return total


def body(activations, out_grad, gate_weights, routes, momentum):
    expert_count = lax.axis_size("expert")
    zlo_count = lax.axis_size("zlo")
    zhi_count = lax.axis_size("zhi")
    z_count = zhi_count * zlo_count
    tokens_here, slots_token, hidden_width = activations.shape
    model_width = out_grad.shape[1]
    own_rows = momentum.shape[0]
    expert_total = EXP_DEV * expert_count
    group_size = zlo_count * 2
    group = ("zlo", "core")

    grad_parts = out_grad.reshape(tokens_here, group_size, own_rows).transpose(1, 0, 2)
    grad_mine = group_exchange(grad_parts, group, group_size)
    grad_mine, activations = lax.optimization_barrier((grad_mine, activations))
    grad_all = lax.all_gather(grad_mine, ("zhi", "expert"), axis=0, tiled=False)
    grad_all = grad_all.reshape(-1, own_rows)

    numbers = jnp.arange(expert_total, dtype=jnp.int32)
    matched = routes[:, :, None] == numbers[None, None, :]
    flat_hidden = activations.reshape(tokens_here * slots_token, hidden_width)
    eye = (
        jnp.arange(tokens_here, dtype=jnp.int32)[:, None, None]
        == jnp.arange(tokens_here, dtype=jnp.int32)[None, :, None]
    )
    selector = (matched.transpose(2, 0, 1)[:, :, None, :] & eye[None]).astype(jnp.bfloat16)
    selector = selector.reshape(expert_total * tokens_here, tokens_here * slots_token)
    chosen = jnp.dot(selector, flat_hidden, preferred_element_type=jnp.float32)
    scale = jnp.sum(jnp.where(matched, gate_weights[:, :, None], 0.0), axis=1)
    scale = scale.T.reshape(expert_total * tokens_here, 1)
    scaled_hidden = (scale * chosen).astype(jnp.bfloat16)
    scaled_hidden = scaled_hidden.reshape(expert_count, EXP_DEV, tokens_here, hidden_width)
    scaled_hidden = scaled_hidden.transpose(1, 0, 2, 3).reshape(expert_total, tokens_here, hidden_width)
    got_hidden = lax.all_to_all(
        scaled_hidden, ("zhi", "expert"), split_axis=0, concat_axis=0, tiled=True
    )
    got_hidden = group_gather(got_hidden, group, group_size)
    got_hidden = got_hidden.transpose(1, 0, 2, 3).reshape(-1, hidden_width)

    gradient = lax.dot_general(
        grad_all, got_hidden, (((0,), (0,)), ((), ())), preferred_element_type=jnp.float32
    )

    new_momentum = MOMENT * momentum + gradient
    ahead = gradient + MOMENT * new_momentum
    square_sum = group_sum(jnp.sum(ahead * ahead), group, group_size)
    norm_value = jnp.sqrt(square_sum)
    scaled = (ahead / (norm_value + EPSILON)).astype(jnp.bfloat16)
    for turn_index in range(NS_ITERS):
        gram = group_sum(gram_of(scaled), group, group_size).astype(jnp.bfloat16)
        scaled = newton_update(scaled, gram)
    update = (math.sqrt(model_width) * scaled.astype(jnp.float32)).astype(jnp.bfloat16)
    return (update, new_momentum)


def solution(mesh):
    dp_count = mesh.shape["dp"]
    expert_count = mesh.shape["expert"]
    group_size = dp_count // EXP_DEV
    zlo = group_size // 2
    zhi = dp_count // 2 // zlo
    devices = np.asarray(mesh.devices).reshape(zhi, zlo, 2, expert_count)
    fine = Mesh(devices, ("zhi", "zlo", "core", "expert"))
    rows = ("zhi", "zlo", "core", "expert")
    cols = ("expert", "zhi", "zlo", "core")
    in_specs = (
        P(rows, None, None),
        P(rows, None),
        P(rows, None),
        P(rows, None),
        P(cols, None),
    )
    out_specs = (P(cols, None), P(cols, None))
    return jax.shard_map(body, mesh=fine, in_specs=in_specs, out_specs=out_specs, check_vma=False)
```

```python
import math

import jax
import jax.numpy as jnp
import numpy as np
from jax import lax
from jax.sharding import Mesh
from jax.sharding import PartitionSpec as P

EXP_DEV = 4
NS_ITERS = 2


MOMENT = 0.95
COEFF_A = 3.4445
COEFF_B = -4.775
COEFF_C = 2.0315
EPSILON = 1e-07


def newton_update(scaled, gram):
    square = jnp.dot(gram, gram, preferred_element_type=jnp.float32)
    poly = (COEFF_B * gram.astype(jnp.float32) + COEFF_C * square).astype(jnp.bfloat16)
    poly = lax.optimization_barrier(poly)
    product = jnp.dot(scaled, poly, preferred_element_type=jnp.float32)
    return (COEFF_A * scaled.astype(jnp.float32) + product).astype(jnp.bfloat16)


def gram_of(scaled):
    return lax.dot_general(
        scaled, scaled, (((0,), (0,)), ((), ())), preferred_element_type=jnp.float32
    )


def group_gather(block, axes, count):
    parts = [block]
    for shift in range(1, count):
        route = [(source, (source + shift) % count) for source in range(count)]
        parts.append(lax.ppermute(block, axes, route))
    return jnp.stack(parts)


def group_exchange(parts, axes, count):
    member = lax.axis_index(axes)
    got = [lax.dynamic_index_in_dim(parts, member, 0, keepdims=False)]
    for shift in range(1, count):
        route = [(source, (source + shift) % count) for source in range(count)]
        send = lax.dynamic_index_in_dim(parts, (member + shift) % count, 0, keepdims=False)
        got.append(lax.ppermute(send, axes, route))
    return jnp.stack(got)


def group_sum(value, axes, count):
    total = value
    for shift in range(1, count):
        route = [(source, (source + shift) % count) for source in range(count)]
        total = total + lax.ppermute(value, axes, route)
    return total


def body(activations, out_grad, gate_weights, routes, momentum):
    expert_count = lax.axis_size("expert")
    zlo_count = lax.axis_size("zlo")
    zhi_count = lax.axis_size("zhi")
    z_count = zhi_count * zlo_count
    tokens_here, slots_token, hidden_width = activations.shape
    model_width = out_grad.shape[1]
    own_rows = momentum.shape[0]
    expert_total = EXP_DEV * expert_count
    group_size = zlo_count * 2
    group = ("zlo", "core")

    grad_parts = out_grad.reshape(tokens_here, group_size, own_rows).transpose(1, 0, 2)
    grad_mine = group_exchange(grad_parts, group, group_size)
    grad_mine, activations = lax.optimization_barrier((grad_mine, activations))
    grad_all = lax.all_gather(grad_mine, ("zhi", "expert"), axis=1, tiled=False)
    grad_all = grad_all.reshape(-1, own_rows)

    numbers = jnp.arange(expert_total, dtype=jnp.int32)
    matched = routes[:, :, None] == numbers[None, None, :]
    flat_hidden = activations.reshape(tokens_here * slots_token, hidden_width)
    eye = (
        jnp.arange(tokens_here, dtype=jnp.int32)[:, None, None]
        == jnp.arange(tokens_here, dtype=jnp.int32)[None, :, None]
    )
    selector = (matched.transpose(2, 0, 1)[:, :, None, :] & eye[None]).astype(jnp.bfloat16)
    selector = selector.reshape(expert_total * tokens_here, tokens_here * slots_token)
    chosen = jnp.dot(selector, flat_hidden, preferred_element_type=jnp.float32)
    scale = jnp.sum(jnp.where(matched, gate_weights[:, :, None], 0.0), axis=1)
    scale = scale.T.reshape(expert_total * tokens_here, 1)
    scaled_hidden = (scale * chosen).astype(jnp.bfloat16)
    scaled_hidden = scaled_hidden.reshape(expert_count, EXP_DEV, tokens_here, hidden_width)
    scaled_hidden = scaled_hidden.transpose(1, 0, 2, 3).reshape(expert_total, tokens_here, hidden_width)
    got_hidden = lax.all_to_all(
        scaled_hidden, ("zhi", "expert"), split_axis=0, concat_axis=0, tiled=True
    )
    got_hidden = group_gather(got_hidden, group, group_size)
    got_hidden = got_hidden.reshape(-1, hidden_width)

    grad_all, got_hidden = lax.optimization_barrier((grad_all, got_hidden))
    gradient = lax.dot_general(
        grad_all, got_hidden, (((0,), (0,)), ((), ())), preferred_element_type=jnp.float32
    )

    new_momentum = MOMENT * momentum + gradient
    ahead = gradient + MOMENT * new_momentum
    square_sum = group_sum(jnp.sum(ahead * ahead), group, group_size)
    norm_value = jnp.sqrt(square_sum)
    scaled = (ahead / (norm_value + EPSILON)).astype(jnp.bfloat16)
    for turn_index in range(NS_ITERS):
        gram = group_sum(gram_of(scaled), group, group_size).astype(jnp.bfloat16)
        scaled = newton_update(scaled, gram)
    update = (math.sqrt(model_width) * scaled.astype(jnp.float32)).astype(jnp.bfloat16)
    return (update, new_momentum)


def solution(mesh):
    dp_count = mesh.shape["dp"]
    expert_count = mesh.shape["expert"]
    group_size = dp_count // EXP_DEV
    zlo = group_size // 2
    zhi = dp_count // 2 // zlo
    devices = np.asarray(mesh.devices).reshape(zhi, zlo, 2, expert_count)
    fine = Mesh(devices, ("zhi", "zlo", "core", "expert"))
    rows = ("zhi", "zlo", "core", "expert")
    cols = ("expert", "zhi", "zlo", "core")
    in_specs = (
        P(rows, None, None),
        P(rows, None),
        P(rows, None),
        P(rows, None),
        P(cols, None),
    )
    out_specs = (P(cols, None), P(cols, None))
    return jax.shard_map(body, mesh=fine, in_specs=in_specs, out_specs=out_specs, check_vma=False)
```

```python
import math

import jax
import jax.numpy as jnp
import numpy as np
from jax import lax
from jax.sharding import Mesh
from jax.sharding import PartitionSpec as P

EXP_DEV = 4
NS_ITERS = 2


MOMENT = 0.95
COEFF_A = 3.4445
COEFF_B = -4.775
COEFF_C = 2.0315
EPSILON = 1e-07


def newton_update(scaled, gram):
    square = jnp.dot(gram, gram, preferred_element_type=jnp.float32)
    poly = (COEFF_B * gram.astype(jnp.float32) + COEFF_C * square).astype(jnp.bfloat16)
    poly = lax.optimization_barrier(poly)
    product = jnp.dot(scaled, poly, preferred_element_type=jnp.float32)
    return (COEFF_A * scaled.astype(jnp.float32) + product).astype(jnp.bfloat16)


def gram_of(scaled):
    return lax.dot_general(
        scaled, scaled, (((0,), (0,)), ((), ())), preferred_element_type=jnp.float32
    )


def group_gather(block, axes, count):
    parts = [block]
    for shift in range(1, count):
        route = [(source, (source + shift) % count) for source in range(count)]
        parts.append(lax.ppermute(block, axes, route))
    return jnp.stack(parts)


def group_exchange(parts, axes, count):
    member = lax.axis_index(axes)
    got = [lax.dynamic_index_in_dim(parts, member, 0, keepdims=False)]
    for shift in range(1, count):
        route = [(source, (source + shift) % count) for source in range(count)]
        send = lax.dynamic_index_in_dim(parts, (member + shift) % count, 0, keepdims=False)
        got.append(lax.ppermute(send, axes, route))
    return jnp.stack(got)


def group_sum(value, axes, count):
    total = value
    for shift in range(1, count):
        route = [(source, (source + shift) % count) for source in range(count)]
        total = total + lax.ppermute(value, axes, route)
    return total


def body(activations, out_grad, gate_weights, routes, momentum):
    expert_count = lax.axis_size("expert")
    zlo_count = lax.axis_size("zlo")
    zhi_count = lax.axis_size("zhi")
    z_count = zhi_count * zlo_count
    tokens_here, slots_token, hidden_width = activations.shape
    model_width = out_grad.shape[1]
    own_rows = momentum.shape[0]
    expert_total = EXP_DEV * expert_count
    group_size = zlo_count * 2
    group = ("zlo", "core")

    grad_parts = out_grad.reshape(tokens_here, group_size, own_rows).transpose(1, 0, 2)
    grad_mine = group_exchange(grad_parts, group, group_size)
    grad_mine, activations = lax.optimization_barrier((grad_mine, activations))
    grad_all = lax.all_gather(grad_mine, ("zhi", "expert"), axis=1, tiled=False)
    grad_all = grad_all.reshape(-1, own_rows)

    numbers = jnp.arange(expert_total, dtype=jnp.int32)
    matched = routes[:, :, None] == numbers[None, None, :]
    flat_hidden = activations.reshape(tokens_here * slots_token, hidden_width)
    eye = (
        jnp.arange(tokens_here, dtype=jnp.int32)[:, None, None]
        == jnp.arange(tokens_here, dtype=jnp.int32)[None, :, None]
    )
    selector = (matched.transpose(2, 0, 1)[:, :, None, :] & eye[None]).astype(jnp.bfloat16)
    selector = selector.reshape(expert_total * tokens_here, tokens_here * slots_token)
    chosen = jnp.dot(selector, flat_hidden, preferred_element_type=jnp.float32)
    scale = jnp.sum(jnp.where(matched, gate_weights[:, :, None], 0.0), axis=1)
    scale = scale.T.reshape(expert_total * tokens_here, 1)
    scaled_hidden = (scale * chosen).astype(jnp.bfloat16)
    scaled_hidden = scaled_hidden.reshape(expert_count, EXP_DEV, tokens_here, hidden_width)
    scaled_hidden = scaled_hidden.transpose(1, 0, 2, 3).reshape(expert_total, tokens_here, hidden_width)
    got_hidden = lax.all_to_all(
        scaled_hidden, ("zhi", "expert"), split_axis=0, concat_axis=0, tiled=True
    )
    got_hidden = group_gather(got_hidden, group, group_size)
    got_hidden = got_hidden.reshape(-1, hidden_width)

    grad_all, got_hidden = lax.optimization_barrier((grad_all, got_hidden))
    gradient = lax.dot_general(
        grad_all, got_hidden, (((0,), (0,)), ((), ())), preferred_element_type=jnp.float32
    )
    gradient = lax.optimization_barrier(gradient)

    new_momentum = MOMENT * momentum + gradient
    ahead = gradient + MOMENT * new_momentum
    square_sum = group_sum(jnp.sum(ahead * ahead), group, group_size)
    norm_value = jnp.sqrt(square_sum)
    scaled = (ahead / (norm_value + EPSILON)).astype(jnp.bfloat16)
    for turn_index in range(NS_ITERS):
        gram = group_sum(gram_of(scaled), group, group_size).astype(jnp.bfloat16)
        scaled = newton_update(scaled, gram)
    update = (math.sqrt(model_width) * scaled.astype(jnp.float32)).astype(jnp.bfloat16)
    return (update, new_momentum)


def solution(mesh):
    dp_count = mesh.shape["dp"]
    expert_count = mesh.shape["expert"]
    group_size = dp_count // EXP_DEV
    zlo = group_size // 2
    zhi = dp_count // 2 // zlo
    devices = np.asarray(mesh.devices).reshape(zhi, zlo, 2, expert_count)
    fine = Mesh(devices, ("zhi", "zlo", "core", "expert"))
    rows = ("zhi", "zlo", "core", "expert")
    cols = ("expert", "zhi", "zlo", "core")
    in_specs = (
        P(rows, None, None),
        P(rows, None),
        P(rows, None),
        P(rows, None),
        P(cols, None),
    )
    out_specs = (P(cols, None), P(cols, None))
    return jax.shard_map(body, mesh=fine, in_specs=in_specs, out_specs=out_specs, check_vma=False)
```

```python
import math

import jax
import jax.numpy as jnp
import numpy as np
from jax import lax
from jax.sharding import Mesh
from jax.sharding import PartitionSpec as P

EXP_DEV = 4
NS_ITERS = 2


MOMENT = 0.95
COEFF_A = 3.4445
COEFF_B = -4.775
COEFF_C = 2.0315
EPSILON = 1e-07


def newton_update(scaled, gram):
    square = jnp.dot(gram, gram, preferred_element_type=jnp.float32)
    poly = (COEFF_B * gram.astype(jnp.float32) + COEFF_C * square).astype(jnp.bfloat16)
    poly = lax.optimization_barrier(poly)
    product = jnp.dot(scaled, poly, preferred_element_type=jnp.float32)
    return (COEFF_A * scaled.astype(jnp.float32) + product).astype(jnp.bfloat16)


def gram_of(scaled):
    return lax.dot_general(
        scaled, scaled, (((0,), (0,)), ((), ())), preferred_element_type=jnp.float32
    )


def group_gather(block, axes, count):
    parts = [block]
    for shift in range(1, count):
        route = [(source, (source + shift) % count) for source in range(count)]
        parts.append(lax.ppermute(block, axes, route))
    return jnp.stack(parts)


def group_exchange(parts, axes, count):
    member = lax.axis_index(axes)
    got = [lax.dynamic_index_in_dim(parts, member, 0, keepdims=False)]
    for shift in range(1, count):
        route = [(source, (source + shift) % count) for source in range(count)]
        send = lax.dynamic_index_in_dim(parts, (member + shift) % count, 0, keepdims=False)
        got.append(lax.ppermute(send, axes, route))
    return jnp.stack(got)


def group_sum(value, axes, count):
    total = value
    for shift in range(1, count):
        route = [(source, (source + shift) % count) for source in range(count)]
        total = total + lax.ppermute(value, axes, route)
    return total


def body(activations, out_grad, gate_weights, routes, momentum):
    expert_count = lax.axis_size("expert")
    zlo_count = lax.axis_size("zlo")
    zhi_count = lax.axis_size("zhi")
    z_count = zhi_count * zlo_count
    tokens_here, slots_token, hidden_width = activations.shape
    model_width = out_grad.shape[1]
    own_rows = momentum.shape[0]
    expert_total = EXP_DEV * expert_count
    group_size = zlo_count * 2
    group = ("zlo", "core")

    grad_parts = out_grad.reshape(tokens_here, group_size, own_rows).transpose(1, 0, 2)
    grad_mine = group_exchange(grad_parts, group, group_size)
    grad_mine, activations = lax.optimization_barrier((grad_mine, activations))
    grad_all = [
        lax.all_gather(grad_mine[shift], ("zhi", "expert"), axis=0, tiled=False)
        for shift in range(group_size)
    ]

    numbers = jnp.arange(expert_total, dtype=jnp.int32)
    matched = routes[:, :, None] == numbers[None, None, :]
    flat_hidden = activations.reshape(tokens_here * slots_token, hidden_width)
    eye = (
        jnp.arange(tokens_here, dtype=jnp.int32)[:, None, None]
        == jnp.arange(tokens_here, dtype=jnp.int32)[None, :, None]
    )
    selector = (matched.transpose(2, 0, 1)[:, :, None, :] & eye[None]).astype(jnp.bfloat16)
    selector = selector.reshape(expert_total * tokens_here, tokens_here * slots_token)
    chosen = jnp.dot(selector, flat_hidden, preferred_element_type=jnp.float32)
    scale = jnp.sum(jnp.where(matched, gate_weights[:, :, None], 0.0), axis=1)
    scale = scale.T.reshape(expert_total * tokens_here, 1)
    scaled_hidden = (scale * chosen).astype(jnp.bfloat16)
    scaled_hidden = scaled_hidden.reshape(expert_count, EXP_DEV, tokens_here, hidden_width)
    scaled_hidden = scaled_hidden.transpose(1, 0, 2, 3).reshape(expert_total, tokens_here, hidden_width)
    got_hidden = lax.all_to_all(
        scaled_hidden, ("zhi", "expert"), split_axis=0, concat_axis=0, tiled=True
    )
    got_hidden = group_gather(got_hidden, group, group_size)

    gradient = None
    for shift in range(group_size):
        grad_part = grad_all[shift].reshape(-1, own_rows)
        hidden_part = got_hidden[shift].reshape(-1, hidden_width)
        grad_part, hidden_part = lax.optimization_barrier((grad_part, hidden_part))
        product = lax.dot_general(
            grad_part, hidden_part, (((0,), (0,)), ((), ())), preferred_element_type=jnp.float32
        )
        gradient = product if gradient is None else gradient + product
    gradient = lax.optimization_barrier(gradient)

    new_momentum = MOMENT * momentum + gradient
    ahead = gradient + MOMENT * new_momentum
    square_sum = group_sum(jnp.sum(ahead * ahead), group, group_size)
    norm_value = jnp.sqrt(square_sum)
    scaled = (ahead / (norm_value + EPSILON)).astype(jnp.bfloat16)
    for turn_index in range(NS_ITERS):
        gram = group_sum(gram_of(scaled), group, group_size).astype(jnp.bfloat16)
        scaled = newton_update(scaled, gram)
    update = (math.sqrt(model_width) * scaled.astype(jnp.float32)).astype(jnp.bfloat16)
    return (update, new_momentum)


def solution(mesh):
    dp_count = mesh.shape["dp"]
    expert_count = mesh.shape["expert"]
    group_size = dp_count // EXP_DEV
    zlo = group_size // 2
    zhi = dp_count // 2 // zlo
    devices = np.asarray(mesh.devices).reshape(zhi, zlo, 2, expert_count)
    fine = Mesh(devices, ("zhi", "zlo", "core", "expert"))
    rows = ("zhi", "zlo", "core", "expert")
    cols = ("expert", "zhi", "zlo", "core")
    in_specs = (
        P(rows, None, None),
        P(rows, None),
        P(rows, None),
        P(rows, None),
        P(cols, None),
    )
    out_specs = (P(cols, None), P(cols, None))
    return jax.shard_map(body, mesh=fine, in_specs=in_specs, out_specs=out_specs, check_vma=False)
```

```python
import math

import jax
import jax.numpy as jnp
import numpy as np
from jax import lax
from jax.sharding import Mesh
from jax.sharding import PartitionSpec as P

EXP_DEV = 4
NS_ITERS = 2


MOMENT = 0.95
COEFF_A = 3.4445
COEFF_B = -4.775
COEFF_C = 2.0315
EPSILON = 1e-07


def newton_update(scaled, gram):
    square = jnp.dot(gram, gram, preferred_element_type=jnp.float32)
    poly = (COEFF_B * gram.astype(jnp.float32) + COEFF_C * square).astype(jnp.bfloat16)
    poly = lax.optimization_barrier(poly)
    product = jnp.dot(scaled, poly, preferred_element_type=jnp.float32)
    return (COEFF_A * scaled.astype(jnp.float32) + product).astype(jnp.bfloat16)


def gram_of(scaled):
    return lax.dot_general(
        scaled, scaled, (((0,), (0,)), ((), ())), preferred_element_type=jnp.float32
    )


def group_gather(block, axes, count):
    parts = [block]
    for shift in range(1, count):
        route = [(source, (source + shift) % count) for source in range(count)]
        parts.append(lax.ppermute(block, axes, route))
    return jnp.stack(parts)


def group_exchange(parts, axes, count):
    member = lax.axis_index(axes)
    got = [lax.dynamic_index_in_dim(parts, member, 0, keepdims=False)]
    for shift in range(1, count):
        route = [(source, (source + shift) % count) for source in range(count)]
        send = lax.dynamic_index_in_dim(parts, (member + shift) % count, 0, keepdims=False)
        got.append(lax.ppermute(send, axes, route))
    return jnp.stack(got)


def group_sum(value, axes, count, wire=None):
    sent = value if wire is None else value.astype(wire)
    total = sent.astype(value.dtype)
    for shift in range(1, count):
        route = [(source, (source + shift) % count) for source in range(count)]
        total = total + lax.ppermute(sent, axes, route).astype(value.dtype)
    return total


def body(activations, out_grad, gate_weights, routes, momentum):
    expert_count = lax.axis_size("expert")
    zlo_count = lax.axis_size("zlo")
    zhi_count = lax.axis_size("zhi")
    z_count = zhi_count * zlo_count
    tokens_here, slots_token, hidden_width = activations.shape
    model_width = out_grad.shape[1]
    own_rows = momentum.shape[0]
    expert_total = EXP_DEV * expert_count
    group_size = zlo_count * 2
    group = ("zlo", "core")

    grad_parts = out_grad.reshape(tokens_here, group_size, own_rows).transpose(1, 0, 2)
    grad_mine = group_exchange(grad_parts, group, group_size)
    grad_mine, activations = lax.optimization_barrier((grad_mine, activations))
    grad_all = lax.all_gather(grad_mine, ("zhi", "expert"), axis=1, tiled=False)
    grad_all = grad_all.reshape(-1, own_rows)

    numbers = jnp.arange(expert_total, dtype=jnp.int32)
    matched = routes[:, :, None] == numbers[None, None, :]
    flat_hidden = activations.reshape(tokens_here * slots_token, hidden_width)
    eye = (
        jnp.arange(tokens_here, dtype=jnp.int32)[:, None, None]
        == jnp.arange(tokens_here, dtype=jnp.int32)[None, :, None]
    )
    selector = (matched.transpose(2, 0, 1)[:, :, None, :] & eye[None]).astype(jnp.bfloat16)
    selector = selector.reshape(expert_total * tokens_here, tokens_here * slots_token)
    chosen = jnp.dot(selector, flat_hidden, preferred_element_type=jnp.float32)
    scale = jnp.sum(jnp.where(matched, gate_weights[:, :, None], 0.0), axis=1)
    scale = scale.T.reshape(expert_total * tokens_here, 1)
    scaled_hidden = (scale * chosen).astype(jnp.bfloat16)
    scaled_hidden = scaled_hidden.reshape(expert_count, EXP_DEV, tokens_here, hidden_width)
    scaled_hidden = scaled_hidden.transpose(1, 0, 2, 3).reshape(expert_total, tokens_here, hidden_width)
    got_hidden = lax.all_to_all(
        scaled_hidden, ("zhi", "expert"), split_axis=0, concat_axis=0, tiled=True
    )
    got_hidden = group_gather(got_hidden, group, group_size)
    got_hidden = got_hidden.reshape(-1, hidden_width)

    grad_all, got_hidden = lax.optimization_barrier((grad_all, got_hidden))
    gradient = lax.dot_general(
        grad_all, got_hidden, (((0,), (0,)), ((), ())), preferred_element_type=jnp.float32
    )
    gradient = lax.optimization_barrier(gradient)

    new_momentum = MOMENT * momentum + gradient
    ahead = gradient + MOMENT * new_momentum
    square_sum = group_sum(jnp.sum(ahead * ahead), group, group_size)
    norm_value = jnp.sqrt(square_sum)
    scaled = (ahead / (norm_value + EPSILON)).astype(jnp.bfloat16)
    for turn_index in range(NS_ITERS):
        gram = group_sum(gram_of(scaled), group, group_size, jnp.bfloat16).astype(jnp.bfloat16)
        scaled = newton_update(scaled, gram)
    update = (math.sqrt(model_width) * scaled.astype(jnp.float32)).astype(jnp.bfloat16)
    return (update, new_momentum)


def solution(mesh):
    dp_count = mesh.shape["dp"]
    expert_count = mesh.shape["expert"]
    group_size = dp_count // EXP_DEV
    zlo = group_size // 2
    zhi = dp_count // 2 // zlo
    devices = np.asarray(mesh.devices).reshape(zhi, zlo, 2, expert_count)
    fine = Mesh(devices, ("zhi", "zlo", "core", "expert"))
    rows = ("zhi", "zlo", "core", "expert")
    cols = ("expert", "zhi", "zlo", "core")
    in_specs = (
        P(rows, None, None),
        P(rows, None),
        P(rows, None),
        P(rows, None),
        P(cols, None),
    )
    out_specs = (P(cols, None), P(cols, None))
    return jax.shard_map(body, mesh=fine, in_specs=in_specs, out_specs=out_specs, check_vma=False)
```

```python
import math

import jax
import jax.numpy as jnp
import numpy as np
from jax import lax
from jax.sharding import Mesh
from jax.sharding import PartitionSpec as P

EXP_DEV = 4
NS_ITERS = 2


MOMENT = 0.95
COEFF_A = 3.4445
COEFF_B = -4.775
COEFF_C = 2.0315
EPSILON = 1e-07


def newton_update(scaled, gram):
    square = jnp.dot(gram, gram, preferred_element_type=jnp.float32)
    poly = (COEFF_B * gram.astype(jnp.float32) + COEFF_C * square).astype(jnp.bfloat16)
    poly = lax.optimization_barrier(poly)
    product = jnp.dot(scaled, poly, preferred_element_type=jnp.float32)
    return (COEFF_A * scaled.astype(jnp.float32) + product).astype(jnp.bfloat16)


def gram_of(scaled):
    return lax.dot_general(
        scaled, scaled, (((0,), (0,)), ((), ())), preferred_element_type=jnp.float32
    )


def group_gather(block, axes, count):
    parts = [block]
    for shift in range(1, count):
        route = [(source, (source + shift) % count) for source in range(count)]
        parts.append(lax.ppermute(block, axes, route))
    return jnp.stack(parts)


def group_exchange(parts, axes, count, axis=0):
    member = lax.axis_index(axes)
    got = [lax.dynamic_index_in_dim(parts, member, axis, keepdims=False)]
    for shift in range(1, count):
        route = [(source, (source + shift) % count) for source in range(count)]
        send = lax.dynamic_index_in_dim(parts, (member + shift) % count, axis, keepdims=False)
        got.append(lax.ppermute(send, axes, route))
    return jnp.stack(got)


def group_sum(value, axes, count, wire=None):
    sent = value if wire is None else value.astype(wire)
    total = sent.astype(value.dtype)
    for shift in range(1, count):
        route = [(source, (source + shift) % count) for source in range(count)]
        total = total + lax.ppermute(sent, axes, route).astype(value.dtype)
    return total


def body(activations, out_grad, gate_weights, routes, momentum):
    expert_count = lax.axis_size("expert")
    zlo_count = lax.axis_size("zlo")
    zhi_count = lax.axis_size("zhi")
    z_count = zhi_count * zlo_count
    tokens_here, slots_token, hidden_width = activations.shape
    model_width = out_grad.shape[1]
    own_rows = momentum.shape[0]
    expert_total = EXP_DEV * expert_count
    group_size = zlo_count * 2
    group = ("zlo", "core")

    grad_parts = out_grad.reshape(tokens_here, group_size, own_rows)
    grad_mine = group_exchange(grad_parts, group, group_size, axis=1)
    grad_mine, activations = lax.optimization_barrier((grad_mine, activations))
    grad_all = lax.all_gather(grad_mine, ("zhi", "expert"), axis=1, tiled=False)
    grad_all = grad_all.reshape(-1, own_rows)

    numbers = jnp.arange(expert_total, dtype=jnp.int32)
    matched = routes[:, :, None] == numbers[None, None, :]
    flat_hidden = activations.reshape(tokens_here * slots_token, hidden_width)
    eye = (
        jnp.arange(tokens_here, dtype=jnp.int32)[:, None, None]
        == jnp.arange(tokens_here, dtype=jnp.int32)[None, :, None]
    )
    selector = (matched.transpose(2, 0, 1)[:, :, None, :] & eye[None]).astype(jnp.bfloat16)
    selector = selector.reshape(expert_total * tokens_here, tokens_here * slots_token)
    chosen = jnp.dot(selector, flat_hidden, preferred_element_type=jnp.float32)
    scale = jnp.sum(jnp.where(matched, gate_weights[:, :, None], 0.0), axis=1)
    scale = scale.T.reshape(expert_total * tokens_here, 1)
    scaled_hidden = (scale * chosen).astype(jnp.bfloat16)
    scaled_hidden = scaled_hidden.reshape(expert_count, EXP_DEV, tokens_here, hidden_width)
    scaled_hidden = scaled_hidden.transpose(1, 0, 2, 3).reshape(expert_total, tokens_here, hidden_width)
    got_hidden = lax.all_to_all(
        scaled_hidden, ("zhi", "expert"), split_axis=0, concat_axis=0, tiled=True
    )
    got_hidden = group_gather(got_hidden, group, group_size)
    got_hidden = got_hidden.reshape(-1, hidden_width)

    grad_all, got_hidden = lax.optimization_barrier((grad_all, got_hidden))
    gradient = lax.dot_general(
        grad_all, got_hidden, (((0,), (0,)), ((), ())), preferred_element_type=jnp.float32
    )
    gradient = lax.optimization_barrier(gradient)

    new_momentum = MOMENT * momentum + gradient
    ahead = gradient + MOMENT * new_momentum
    square_sum = group_sum(jnp.sum(ahead * ahead), group, group_size)
    norm_value = jnp.sqrt(square_sum)
    scaled = (ahead / (norm_value + EPSILON)).astype(jnp.bfloat16)
    for turn_index in range(NS_ITERS):
        gram = group_sum(gram_of(scaled), group, group_size, jnp.bfloat16).astype(jnp.bfloat16)
        scaled = newton_update(scaled, gram)
    update = (math.sqrt(model_width) * scaled.astype(jnp.float32)).astype(jnp.bfloat16)
    return (update, new_momentum)


def solution(mesh):
    dp_count = mesh.shape["dp"]
    expert_count = mesh.shape["expert"]
    group_size = dp_count // EXP_DEV
    zlo = group_size // 2
    zhi = dp_count // 2 // zlo
    devices = np.asarray(mesh.devices).reshape(zhi, zlo, 2, expert_count)
    fine = Mesh(devices, ("zhi", "zlo", "core", "expert"))
    rows = ("zhi", "zlo", "core", "expert")
    cols = ("expert", "zhi", "zlo", "core")
    in_specs = (
        P(rows, None, None),
        P(rows, None),
        P(rows, None),
        P(rows, None),
        P(cols, None),
    )
    out_specs = (P(cols, None), P(cols, None))
    return jax.shard_map(body, mesh=fine, in_specs=in_specs, out_specs=out_specs, check_vma=False)
```

```python
import math

import jax
import jax.numpy as jnp
import numpy as np
from jax import lax
from jax.sharding import Mesh
from jax.sharding import PartitionSpec as P

EXP_DEV = 4
NS_ITERS = 2


MOMENT = 0.95
COEFF_A = 3.4445
COEFF_B = -4.775
COEFF_C = 2.0315
EPSILON = 1e-07


def newton_update(scaled, gram):
    square = jnp.dot(gram, gram, preferred_element_type=jnp.float32)
    poly = (COEFF_B * gram.astype(jnp.float32) + COEFF_C * square).astype(jnp.bfloat16)
    poly = lax.optimization_barrier(poly)
    product = jnp.dot(scaled, poly, preferred_element_type=jnp.float32)
    return (COEFF_A * scaled.astype(jnp.float32) + product).astype(jnp.bfloat16)


def gram_of(scaled):
    return lax.dot_general(
        scaled, scaled, (((0,), (0,)), ((), ())), preferred_element_type=jnp.float32
    )


def group_gather(block, axes, count):
    parts = [block]
    for shift in range(1, count):
        route = [(source, (source + shift) % count) for source in range(count)]
        parts.append(lax.ppermute(block, axes, route))
    return jnp.stack(parts)


def pick(parts, index):
    chosen = parts[0]
    for place in range(1, len(parts)):
        chosen = jnp.where(index == place, parts[place], chosen)
    return chosen


def group_exchange(parts, axes, count):
    member = lax.axis_index(axes)
    got = [pick(parts, member)]
    for shift in range(1, count):
        route = [(source, (source + shift) % count) for source in range(count)]
        send = pick(parts, (member + shift) % count)
        got.append(lax.ppermute(send, axes, route))
    return jnp.stack(got)


def group_sum(value, axes, count, wire=None):
    sent = value if wire is None else value.astype(wire)
    total = sent.astype(value.dtype)
    for shift in range(1, count):
        route = [(source, (source + shift) % count) for source in range(count)]
        total = total + lax.ppermute(sent, axes, route).astype(value.dtype)
    return total


def body(activations, out_grad, gate_weights, routes, momentum):
    expert_count = lax.axis_size("expert")
    zlo_count = lax.axis_size("zlo")
    zhi_count = lax.axis_size("zhi")
    z_count = zhi_count * zlo_count
    tokens_here, slots_token, hidden_width = activations.shape
    model_width = out_grad.shape[1]
    own_rows = momentum.shape[0]
    expert_total = EXP_DEV * expert_count
    group_size = zlo_count * 2
    group = ("zlo", "core")

    grad_parts = [out_grad[:, part * own_rows:(part + 1) * own_rows] for part in range(group_size)]
    grad_mine = group_exchange(grad_parts, group, group_size)
    grad_mine, activations = lax.optimization_barrier((grad_mine, activations))
    grad_all = lax.all_gather(grad_mine, ("zhi", "expert"), axis=1, tiled=False)
    grad_all = grad_all.reshape(-1, own_rows)

    numbers = jnp.arange(expert_total, dtype=jnp.int32)
    matched = routes[:, :, None] == numbers[None, None, :]
    flat_hidden = activations.reshape(tokens_here * slots_token, hidden_width)
    eye = (
        jnp.arange(tokens_here, dtype=jnp.int32)[:, None, None]
        == jnp.arange(tokens_here, dtype=jnp.int32)[None, :, None]
    )
    selector = (matched.transpose(2, 0, 1)[:, :, None, :] & eye[None]).astype(jnp.bfloat16)
    selector = selector.reshape(expert_total * tokens_here, tokens_here * slots_token)
    chosen = jnp.dot(selector, flat_hidden, preferred_element_type=jnp.float32)
    scale = jnp.sum(jnp.where(matched, gate_weights[:, :, None], 0.0), axis=1)
    scale = scale.T.reshape(expert_total * tokens_here, 1)
    scaled_hidden = (scale * chosen).astype(jnp.bfloat16)
    scaled_hidden = scaled_hidden.reshape(expert_count, EXP_DEV, tokens_here, hidden_width)
    scaled_hidden = scaled_hidden.transpose(1, 0, 2, 3).reshape(expert_total, tokens_here, hidden_width)
    got_hidden = lax.all_to_all(
        scaled_hidden, ("zhi", "expert"), split_axis=0, concat_axis=0, tiled=True
    )
    got_hidden = group_gather(got_hidden, group, group_size)
    got_hidden = got_hidden.reshape(-1, hidden_width)

    grad_all, got_hidden = lax.optimization_barrier((grad_all, got_hidden))
    gradient = lax.dot_general(
        grad_all, got_hidden, (((0,), (0,)), ((), ())), preferred_element_type=jnp.float32
    )
    gradient = lax.optimization_barrier(gradient)

    new_momentum = MOMENT * momentum + gradient
    ahead = gradient + MOMENT * new_momentum
    square_sum = group_sum(jnp.sum(ahead * ahead), group, group_size)
    norm_value = jnp.sqrt(square_sum)
    scaled = (ahead / (norm_value + EPSILON)).astype(jnp.bfloat16)
    for turn_index in range(NS_ITERS):
        gram = group_sum(gram_of(scaled), group, group_size, jnp.bfloat16).astype(jnp.bfloat16)
        scaled = newton_update(scaled, gram)
    update = (math.sqrt(model_width) * scaled.astype(jnp.float32)).astype(jnp.bfloat16)
    return (update, new_momentum)


def solution(mesh):
    dp_count = mesh.shape["dp"]
    expert_count = mesh.shape["expert"]
    group_size = dp_count // EXP_DEV
    zlo = group_size // 2
    zhi = dp_count // 2 // zlo
    devices = np.asarray(mesh.devices).reshape(zhi, zlo, 2, expert_count)
    fine = Mesh(devices, ("zhi", "zlo", "core", "expert"))
    rows = ("zhi", "zlo", "core", "expert")
    cols = ("expert", "zhi", "zlo", "core")
    in_specs = (
        P(rows, None, None),
        P(rows, None),
        P(rows, None),
        P(rows, None),
        P(cols, None),
    )
    out_specs = (P(cols, None), P(cols, None))
    return jax.shard_map(body, mesh=fine, in_specs=in_specs, out_specs=out_specs, check_vma=False)
```

```python
import math

import jax
import jax.numpy as jnp
import numpy as np
from jax import lax
from jax.sharding import Mesh
from jax.sharding import PartitionSpec as P

EXP_DEV = 4
NS_ITERS = 2


MOMENT = 0.95
COEFF_A = 3.4445
COEFF_B = -4.775
COEFF_C = 2.0315
EPSILON = 1e-07


def newton_update(scaled, gram):
    square = jnp.dot(gram, gram, preferred_element_type=jnp.float32)
    poly = (COEFF_B * gram.astype(jnp.float32) + COEFF_C * square).astype(jnp.bfloat16)
    poly = lax.optimization_barrier(poly)
    product = jnp.dot(scaled, poly, preferred_element_type=jnp.float32)
    return (COEFF_A * scaled.astype(jnp.float32) + product).astype(jnp.bfloat16)


def gram_of(scaled):
    return lax.dot_general(
        scaled, scaled, (((0,), (0,)), ((), ())), preferred_element_type=jnp.float32
    )


def group_gather(block, axes, count):
    parts = [block]
    for shift in range(1, count):
        route = [(source, (source + shift) % count) for source in range(count)]
        parts.append(lax.ppermute(block, axes, route))
    return jnp.stack(parts)


def group_exchange(parts, axes, count):
    member = lax.axis_index(axes)
    got = [lax.dynamic_index_in_dim(parts, member, 0, keepdims=False)]
    for shift in range(1, count):
        route = [(source, (source + shift) % count) for source in range(count)]
        send = lax.dynamic_index_in_dim(parts, (member + shift) % count, 0, keepdims=False)
        got.append(lax.ppermute(send, axes, route))
    return jnp.stack(got)


def group_sum(value, axes, count, wire=None):
    sent = value if wire is None else value.astype(wire)
    total = sent.astype(value.dtype)
    for shift in range(1, count):
        route = [(source, (source + shift) % count) for source in range(count)]
        total = total + lax.ppermute(sent, axes, route).astype(value.dtype)
    return total


def body(activations, out_grad, gate_weights, routes, momentum):
    expert_count = lax.axis_size("expert")
    zlo_count = lax.axis_size("zlo")
    zhi_count = lax.axis_size("zhi")
    z_count = zhi_count * zlo_count
    tokens_here, slots_token, hidden_width = activations.shape
    model_width = out_grad.shape[1]
    own_rows = momentum.shape[0]
    expert_total = EXP_DEV * expert_count
    group_size = zlo_count * 2
    group = ("zlo", "core")

    grad_parts = out_grad.reshape(tokens_here, group_size, own_rows).transpose(1, 0, 2)
    grad_mine = group_exchange(grad_parts, group, group_size)
    grad_mine, activations = lax.optimization_barrier((grad_mine, activations))
    grad_all = lax.all_gather(grad_mine, ("zhi", "expert"), axis=1, tiled=False)
    grad_all = grad_all.reshape(-1, own_rows)

    numbers = jnp.arange(expert_total, dtype=jnp.int32)
    matched = routes[:, :, None] == numbers[None, None, :]
    flat_hidden = activations.reshape(tokens_here * slots_token, hidden_width)
    eye = (
        jnp.arange(tokens_here, dtype=jnp.int32)[:, None, None]
        == jnp.arange(tokens_here, dtype=jnp.int32)[None, :, None]
    )
    selector = (matched.transpose(2, 0, 1)[:, :, None, :] & eye[None]).astype(jnp.bfloat16)
    selector = selector.reshape(expert_total * tokens_here, tokens_here * slots_token)
    chosen = jnp.dot(selector, flat_hidden, preferred_element_type=jnp.float32)
    scale = jnp.sum(jnp.where(matched, gate_weights[:, :, None], 0.0), axis=1)
    scale = scale.T.reshape(expert_total * tokens_here, 1)
    scaled_hidden = (scale * chosen).astype(jnp.bfloat16)
    scaled_hidden = scaled_hidden.reshape(expert_count, EXP_DEV, tokens_here, hidden_width)
    scaled_hidden = scaled_hidden.transpose(1, 0, 2, 3).reshape(expert_total, tokens_here, hidden_width)
    got_hidden = lax.all_to_all(
        scaled_hidden, ("zhi", "expert"), split_axis=0, concat_axis=0, tiled=True
    )
    got_hidden = group_gather(got_hidden, group, group_size)
    got_hidden = got_hidden.reshape(-1, hidden_width)

    grad_all, got_hidden = lax.optimization_barrier((grad_all, got_hidden))
    gradient = lax.dot_general(
        grad_all, got_hidden, (((0,), (0,)), ((), ())), preferred_element_type=jnp.float32
    )
    gradient = lax.optimization_barrier(gradient)

    new_momentum = MOMENT * momentum + gradient
    ahead = gradient + MOMENT * new_momentum
    ahead, own_square_sum = lax.optimization_barrier((ahead, jnp.sum(ahead * ahead)))
    square_sum = group_sum(own_square_sum, group, group_size)
    norm_value = jnp.sqrt(square_sum)
    scaled = (ahead / (norm_value + EPSILON)).astype(jnp.bfloat16)
    for turn_index in range(NS_ITERS):
        gram = group_sum(gram_of(scaled), group, group_size, jnp.bfloat16).astype(jnp.bfloat16)
        scaled = newton_update(scaled, gram)
    update = (math.sqrt(model_width) * scaled.astype(jnp.float32)).astype(jnp.bfloat16)
    return (update, new_momentum)


def solution(mesh):
    dp_count = mesh.shape["dp"]
    expert_count = mesh.shape["expert"]
    group_size = dp_count // EXP_DEV
    zlo = group_size // 2
    zhi = dp_count // 2 // zlo
    devices = np.asarray(mesh.devices).reshape(zhi, zlo, 2, expert_count)
    fine = Mesh(devices, ("zhi", "zlo", "core", "expert"))
    rows = ("zhi", "zlo", "core", "expert")
    cols = ("expert", "zhi", "zlo", "core")
    in_specs = (
        P(rows, None, None),
        P(rows, None),
        P(rows, None),
        P(rows, None),
        P(cols, None),
    )
    out_specs = (P(cols, None), P(cols, None))
    return jax.shard_map(body, mesh=fine, in_specs=in_specs, out_specs=out_specs, check_vma=False)
```

```python
import math

import jax
import jax.numpy as jnp
import numpy as np
from jax import lax
from jax.sharding import Mesh
from jax.sharding import PartitionSpec as P

EXP_DEV = 4
NS_ITERS = 2


MOMENT = 0.95
COEFF_A = 3.4445
COEFF_B = -4.775
COEFF_C = 2.0315
EPSILON = 1e-07


def newton_update(scaled, gram):
    square = jnp.dot(gram, gram, preferred_element_type=jnp.float32)
    poly = (COEFF_B * gram.astype(jnp.float32) + COEFF_C * square).astype(jnp.bfloat16)
    poly = lax.optimization_barrier(poly)
    product = jnp.dot(scaled, poly, preferred_element_type=jnp.float32)
    return (COEFF_A * scaled.astype(jnp.float32) + product).astype(jnp.bfloat16)


def gram_of(scaled):
    return lax.dot_general(
        scaled, scaled, (((0,), (0,)), ((), ())), preferred_element_type=jnp.float32
    )


def group_gather(block, axes, count):
    parts = [block]
    for shift in range(1, count):
        route = [(source, (source + shift) % count) for source in range(count)]
        parts.append(lax.ppermute(block, axes, route))
    return jnp.stack(parts)


def group_exchange(parts, axes, count):
    member = lax.axis_index(axes)
    got = [lax.dynamic_index_in_dim(parts, member, 0, keepdims=False)]
    for shift in range(1, count):
        route = [(source, (source + shift) % count) for source in range(count)]
        send = lax.dynamic_index_in_dim(parts, (member + shift) % count, 0, keepdims=False)
        got.append(lax.ppermute(send, axes, route))
    return jnp.stack(got)


def group_sum(value, axes, count, wire=None):
    sent = value if wire is None else value.astype(wire)
    total = sent.astype(value.dtype)
    for shift in range(1, count):
        route = [(source, (source + shift) % count) for source in range(count)]
        total = total + lax.ppermute(sent, axes, route).astype(value.dtype)
    return total


def body(activations, out_grad, gate_weights, routes, momentum):
    expert_count = lax.axis_size("expert")
    zlo_count = lax.axis_size("zlo")
    zhi_count = lax.axis_size("zhi")
    z_count = zhi_count * zlo_count
    tokens_here, slots_token, hidden_width = activations.shape
    model_width = out_grad.shape[1]
    own_rows = momentum.shape[0]
    expert_total = EXP_DEV * expert_count
    group_size = zlo_count * 2
    group = ("zlo", "core")

    grad_parts = out_grad.reshape(tokens_here, group_size, own_rows).transpose(1, 0, 2)
    grad_mine = group_exchange(grad_parts, group, group_size)
    grad_mine, activations = lax.optimization_barrier((grad_mine, activations))
    grad_all = lax.all_gather(grad_mine, ("zhi", "expert"), axis=1, tiled=False)
    grad_all = grad_all.reshape(-1, own_rows)

    numbers = jnp.arange(expert_total, dtype=jnp.int32)
    matched = routes[:, :, None] == numbers[None, None, :]
    flat_hidden = activations.reshape(tokens_here * slots_token, hidden_width)
    eye = (
        jnp.arange(tokens_here, dtype=jnp.int32)[:, None, None]
        == jnp.arange(tokens_here, dtype=jnp.int32)[None, :, None]
    )
    selector = (matched.transpose(2, 0, 1)[:, :, None, :] & eye[None]).astype(jnp.bfloat16)
    selector = selector.reshape(expert_total * tokens_here, tokens_here * slots_token)
    chosen = jnp.dot(selector, flat_hidden, preferred_element_type=jnp.float32)
    scale = jnp.sum(jnp.where(matched, gate_weights[:, :, None], 0.0), axis=1)
    scale = scale.T.reshape(expert_total * tokens_here, 1)
    scaled_hidden = (scale * chosen).astype(jnp.bfloat16)
    scaled_hidden = scaled_hidden.reshape(expert_count, EXP_DEV, tokens_here, hidden_width)
    scaled_hidden = scaled_hidden.transpose(1, 0, 2, 3).reshape(expert_total, tokens_here, hidden_width)
    got_hidden = lax.all_to_all(
        scaled_hidden, ("zhi", "expert"), split_axis=0, concat_axis=0, tiled=True
    )
    got_hidden = group_gather(got_hidden, group, group_size)
    got_hidden = got_hidden.reshape(-1, hidden_width)

    grad_all, got_hidden = lax.optimization_barrier((grad_all, got_hidden))
    gradient = lax.dot_general(
        got_hidden, grad_all, (((0,), (0,)), ((), ())), preferred_element_type=jnp.float32
    ).T
    gradient = lax.optimization_barrier(gradient)

    new_momentum = MOMENT * momentum + gradient
    ahead = gradient + MOMENT * new_momentum
    square_sum = group_sum(jnp.sum(ahead * ahead), group, group_size)
    norm_value = jnp.sqrt(square_sum)
    scaled = (ahead / (norm_value + EPSILON)).astype(jnp.bfloat16)
    for turn_index in range(NS_ITERS):
        gram = group_sum(gram_of(scaled), group, group_size, jnp.bfloat16).astype(jnp.bfloat16)
        scaled = newton_update(scaled, gram)
    update = (math.sqrt(model_width) * scaled.astype(jnp.float32)).astype(jnp.bfloat16)
    return (update, new_momentum)


def solution(mesh):
    dp_count = mesh.shape["dp"]
    expert_count = mesh.shape["expert"]
    group_size = dp_count // EXP_DEV
    zlo = group_size // 2
    zhi = dp_count // 2 // zlo
    devices = np.asarray(mesh.devices).reshape(zhi, zlo, 2, expert_count)
    fine = Mesh(devices, ("zhi", "zlo", "core", "expert"))
    rows = ("zhi", "zlo", "core", "expert")
    cols = ("expert", "zhi", "zlo", "core")
    in_specs = (
        P(rows, None, None),
        P(rows, None),
        P(rows, None),
        P(rows, None),
        P(cols, None),
    )
    out_specs = (P(cols, None), P(cols, None))
    return jax.shard_map(body, mesh=fine, in_specs=in_specs, out_specs=out_specs, check_vma=False)
```

```python
import math

import jax
import jax.numpy as jnp
import numpy as np
from jax import lax
from jax.sharding import Mesh
from jax.sharding import PartitionSpec as P

EXP_DEV = 4
NS_ITERS = 2


MOMENT = 0.95
COEFF_A = 3.4445
COEFF_B = -4.775
COEFF_C = 2.0315
EPSILON = 1e-07


def newton_update(scaled, gram):
    square = jnp.dot(gram, gram, preferred_element_type=jnp.float32)
    poly = (COEFF_B * gram.astype(jnp.float32) + COEFF_C * square).astype(jnp.bfloat16)
    poly = lax.optimization_barrier(poly)
    product = jnp.dot(scaled, poly, preferred_element_type=jnp.float32)
    return (COEFF_A * scaled.astype(jnp.float32) + product).astype(jnp.bfloat16)


def gram_of(scaled):
    return lax.dot_general(
        scaled, scaled, (((0,), (0,)), ((), ())), preferred_element_type=jnp.float32
    )


def group_gather(block, axes, count):
    parts = [block]
    for shift in range(1, count):
        route = [(source, (source + shift) % count) for source in range(count)]
        parts.append(lax.ppermute(block, axes, route))
    return jnp.stack(parts)


def group_exchange(parts, axes, count):
    member = lax.axis_index(axes)
    got = [lax.dynamic_index_in_dim(parts, member, 0, keepdims=False)]
    for shift in range(1, count):
        route = [(source, (source + shift) % count) for source in range(count)]
        send = lax.dynamic_index_in_dim(parts, (member + shift) % count, 0, keepdims=False)
        got.append(lax.ppermute(send, axes, route))
    return jnp.stack(got)


def group_sum(value, axes, count, wire=None):
    sent = value if wire is None else value.astype(wire)
    total = sent.astype(value.dtype)
    for shift in range(1, count):
        route = [(source, (source + shift) % count) for source in range(count)]
        total = total + lax.ppermute(sent, axes, route).astype(value.dtype)
    return total


def body(activations, out_grad, gate_weights, routes, momentum):
    expert_count = lax.axis_size("expert")
    zlo_count = lax.axis_size("zlo")
    zhi_count = lax.axis_size("zhi")
    z_count = zhi_count * zlo_count
    tokens_here, slots_token, hidden_width = activations.shape
    model_width = out_grad.shape[1]
    own_rows = momentum.shape[0]
    expert_total = EXP_DEV * expert_count
    group_size = zlo_count * 2
    group = ("zlo", "core")

    grad_parts = out_grad.reshape(tokens_here, group_size, own_rows).transpose(1, 0, 2)
    grad_mine = group_exchange(grad_parts, group, group_size)
    grad_mine, activations = lax.optimization_barrier((grad_mine, activations))
    grad_all = lax.all_gather(grad_mine, ("zhi", "expert"), axis=1, tiled=False)
    grad_all = grad_all.reshape(-1, own_rows)

    numbers = jnp.arange(expert_total, dtype=jnp.int32)
    matched = routes[:, :, None] == numbers[None, None, :]
    flat_hidden = activations.reshape(tokens_here * slots_token, hidden_width)
    eye = (
        jnp.arange(tokens_here, dtype=jnp.int32)[:, None, None]
        == jnp.arange(tokens_here, dtype=jnp.int32)[None, :, None]
    )
    selector = (matched.transpose(2, 0, 1)[:, :, None, :] & eye[None]).astype(jnp.bfloat16)
    selector = selector.reshape(expert_total * tokens_here, tokens_here * slots_token)
    chosen = jnp.dot(selector, flat_hidden, preferred_element_type=jnp.float32)
    scale = jnp.sum(jnp.where(matched, gate_weights[:, :, None], 0.0), axis=1)
    scale = scale.T.reshape(expert_total * tokens_here, 1)
    scaled_hidden = (scale * chosen).astype(jnp.bfloat16)
    scaled_hidden = scaled_hidden.reshape(expert_count, EXP_DEV, tokens_here, hidden_width)
    scaled_hidden = scaled_hidden.transpose(1, 0, 2, 3).reshape(expert_total, tokens_here, hidden_width)
    got_hidden = lax.all_to_all(
        scaled_hidden, ("zhi", "expert"), split_axis=0, concat_axis=0, tiled=True
    )
    got_hidden = group_gather(got_hidden, group, group_size)
    got_hidden = got_hidden.reshape(-1, hidden_width)

    grad_all, got_hidden = lax.optimization_barrier((grad_all, got_hidden))
    gradient = lax.dot_general(
        grad_all, got_hidden, (((0,), (0,)), ((), ())), preferred_element_type=jnp.float32
    )
    gradient = lax.optimization_barrier(gradient)

    new_momentum = MOMENT * momentum + gradient
    ahead = gradient + MOMENT * new_momentum
    square_sum = group_sum(jnp.sum(ahead * ahead), group, group_size)
    raw_gram = group_sum(gram_of(ahead.astype(jnp.bfloat16)), group, group_size, jnp.bfloat16)
    norm_value = jnp.sqrt(square_sum)
    scaled = (ahead / (norm_value + EPSILON)).astype(jnp.bfloat16)
    inverse = 1.0 / (norm_value + EPSILON)
    for turn_index in range(NS_ITERS):
        if turn_index == 0:
            gram = (raw_gram * (inverse * inverse)).astype(jnp.bfloat16)
        else:
            gram = group_sum(gram_of(scaled), group, group_size, jnp.bfloat16).astype(jnp.bfloat16)
        scaled = newton_update(scaled, gram)
    update = (math.sqrt(model_width) * scaled.astype(jnp.float32)).astype(jnp.bfloat16)
    return (update, new_momentum)


def solution(mesh):
    dp_count = mesh.shape["dp"]
    expert_count = mesh.shape["expert"]
    group_size = dp_count // EXP_DEV
    zlo = group_size // 2
    zhi = dp_count // 2 // zlo
    devices = np.asarray(mesh.devices).reshape(zhi, zlo, 2, expert_count)
    fine = Mesh(devices, ("zhi", "zlo", "core", "expert"))
    rows = ("zhi", "zlo", "core", "expert")
    cols = ("expert", "zhi", "zlo", "core")
    in_specs = (
        P(rows, None, None),
        P(rows, None),
        P(rows, None),
        P(rows, None),
        P(cols, None),
    )
    out_specs = (P(cols, None), P(cols, None))
    return jax.shard_map(body, mesh=fine, in_specs=in_specs, out_specs=out_specs, check_vma=False)
```

```python
import math

import jax
import jax.numpy as jnp
import numpy as np
from jax import lax
from jax.sharding import Mesh
from jax.sharding import PartitionSpec as P

EXP_DEV = 4
NS_ITERS = 2


MOMENT = 0.95
COEFF_A = 3.4445
COEFF_B = -4.775
COEFF_C = 2.0315
EPSILON = 1e-07


def newton_update(scaled, gram):
    square = jnp.dot(gram, gram, preferred_element_type=jnp.float32)
    poly = (COEFF_B * gram.astype(jnp.float32) + COEFF_C * square).astype(jnp.bfloat16)
    poly = lax.optimization_barrier(poly)
    product = jnp.dot(scaled, poly, preferred_element_type=jnp.float32)
    return (COEFF_A * scaled.astype(jnp.float32) + product).astype(jnp.bfloat16)


def gram_of(scaled):
    return lax.dot_general(
        scaled, scaled, (((0,), (0,)), ((), ())), preferred_element_type=jnp.float32
    )


def gram_sum(scaled, axes, count):
    width = scaled.shape[1]
    halves = []
    for begin in (0, width // 2):
        part = lax.dot_general(
            scaled, scaled[:, begin:begin + width // 2], (((0,), (0,)), ((), ())),
            preferred_element_type=jnp.float32,
        )
        halves.append(group_sum(part, axes, count, jnp.bfloat16))
    return jnp.concatenate(halves, axis=1)


def group_gather(block, axes, count):
    parts = [block]
    for shift in range(1, count):
        route = [(source, (source + shift) % count) for source in range(count)]
        parts.append(lax.ppermute(block, axes, route))
    return jnp.stack(parts)


def group_exchange(parts, axes, count):
    member = lax.axis_index(axes)
    got = [lax.dynamic_index_in_dim(parts, member, 0, keepdims=False)]
    for shift in range(1, count):
        route = [(source, (source + shift) % count) for source in range(count)]
        send = lax.dynamic_index_in_dim(parts, (member + shift) % count, 0, keepdims=False)
        got.append(lax.ppermute(send, axes, route))
    return jnp.stack(got)


def group_sum(value, axes, count, wire=None):
    sent = value if wire is None else value.astype(wire)
    total = sent.astype(value.dtype)
    for shift in range(1, count):
        route = [(source, (source + shift) % count) for source in range(count)]
        total = total + lax.ppermute(sent, axes, route).astype(value.dtype)
    return total


def body(activations, out_grad, gate_weights, routes, momentum):
    expert_count = lax.axis_size("expert")
    zlo_count = lax.axis_size("zlo")
    zhi_count = lax.axis_size("zhi")
    z_count = zhi_count * zlo_count
    tokens_here, slots_token, hidden_width = activations.shape
    model_width = out_grad.shape[1]
    own_rows = momentum.shape[0]
    expert_total = EXP_DEV * expert_count
    group_size = zlo_count * 2
    group = ("zlo", "core")

    grad_parts = out_grad.reshape(tokens_here, group_size, own_rows).transpose(1, 0, 2)
    grad_mine = group_exchange(grad_parts, group, group_size)
    grad_mine, activations = lax.optimization_barrier((grad_mine, activations))
    grad_all = lax.all_gather(grad_mine, ("zhi", "expert"), axis=1, tiled=False)
    grad_all = grad_all.reshape(-1, own_rows)

    numbers = jnp.arange(expert_total, dtype=jnp.int32)
    matched = routes[:, :, None] == numbers[None, None, :]
    flat_hidden = activations.reshape(tokens_here * slots_token, hidden_width)
    eye = (
        jnp.arange(tokens_here, dtype=jnp.int32)[:, None, None]
        == jnp.arange(tokens_here, dtype=jnp.int32)[None, :, None]
    )
    selector = (matched.transpose(2, 0, 1)[:, :, None, :] & eye[None]).astype(jnp.bfloat16)
    selector = selector.reshape(expert_total * tokens_here, tokens_here * slots_token)
    chosen = jnp.dot(selector, flat_hidden, preferred_element_type=jnp.float32)
    scale = jnp.sum(jnp.where(matched, gate_weights[:, :, None], 0.0), axis=1)
    scale = scale.T.reshape(expert_total * tokens_here, 1)
    scaled_hidden = (scale * chosen).astype(jnp.bfloat16)
    scaled_hidden = scaled_hidden.reshape(expert_count, EXP_DEV, tokens_here, hidden_width)
    scaled_hidden = scaled_hidden.transpose(1, 0, 2, 3).reshape(expert_total, tokens_here, hidden_width)
    got_hidden = lax.all_to_all(
        scaled_hidden, ("zhi", "expert"), split_axis=0, concat_axis=0, tiled=True
    )
    got_hidden = group_gather(got_hidden, group, group_size)
    got_hidden = got_hidden.reshape(-1, hidden_width)

    grad_all, got_hidden = lax.optimization_barrier((grad_all, got_hidden))
    gradient = lax.dot_general(
        grad_all, got_hidden, (((0,), (0,)), ((), ())), preferred_element_type=jnp.float32
    )
    gradient = lax.optimization_barrier(gradient)

    new_momentum = MOMENT * momentum + gradient
    ahead = gradient + MOMENT * new_momentum
    square_sum = group_sum(jnp.sum(ahead * ahead), group, group_size)
    raw_gram = gram_sum(ahead.astype(jnp.bfloat16), group, group_size)
    norm_value = jnp.sqrt(square_sum)
    scaled = (ahead / (norm_value + EPSILON)).astype(jnp.bfloat16)
    inverse = 1.0 / (norm_value + EPSILON)
    for turn_index in range(NS_ITERS):
        if turn_index == 0:
            gram = (raw_gram * (inverse * inverse)).astype(jnp.bfloat16)
        else:
            gram = gram_sum(scaled, group, group_size).astype(jnp.bfloat16)
        scaled = newton_update(scaled, gram)
    update = (math.sqrt(model_width) * scaled.astype(jnp.float32)).astype(jnp.bfloat16)
    return (update, new_momentum)


def solution(mesh):
    dp_count = mesh.shape["dp"]
    expert_count = mesh.shape["expert"]
    group_size = dp_count // EXP_DEV
    zlo = group_size // 2
    zhi = dp_count // 2 // zlo
    devices = np.asarray(mesh.devices).reshape(zhi, zlo, 2, expert_count)
    fine = Mesh(devices, ("zhi", "zlo", "core", "expert"))
    rows = ("zhi", "zlo", "core", "expert")
    cols = ("expert", "zhi", "zlo", "core")
    in_specs = (
        P(rows, None, None),
        P(rows, None),
        P(rows, None),
        P(rows, None),
        P(cols, None),
    )
    out_specs = (P(cols, None), P(cols, None))
    return jax.shard_map(body, mesh=fine, in_specs=in_specs, out_specs=out_specs, check_vma=False)
```

```python
import math

import jax
import jax.numpy as jnp
import numpy as np
from jax import lax
from jax.sharding import Mesh
from jax.sharding import PartitionSpec as P

EXP_DEV = 4
NS_ITERS = 2


MOMENT = 0.95
COEFF_A = 3.4445
COEFF_B = -4.775
COEFF_C = 2.0315
EPSILON = 1e-07


def newton_update(scaled, gram):
    square = jnp.dot(gram, gram, preferred_element_type=jnp.float32)
    poly = (COEFF_B * gram.astype(jnp.float32) + COEFF_C * square).astype(jnp.bfloat16)
    poly = lax.optimization_barrier(poly)
    product = jnp.dot(scaled, poly, preferred_element_type=jnp.float32)
    return (COEFF_A * scaled.astype(jnp.float32) + product).astype(jnp.bfloat16)


def gram_of(scaled):
    return lax.dot_general(
        scaled, scaled, (((0,), (0,)), ((), ())), preferred_element_type=jnp.float32
    )


def group_gather(block, axes, count):
    parts = [block]
    for shift in range(1, count):
        route = [(source, (source + shift) % count) for source in range(count)]
        parts.append(lax.ppermute(block, axes, route))
    return jnp.stack(parts)


def group_exchange(parts, axes, count):
    member = lax.axis_index(axes)
    got = [lax.dynamic_index_in_dim(parts, member, 0, keepdims=False)]
    for shift in range(1, count):
        route = [(source, (source + shift) % count) for source in range(count)]
        send = lax.dynamic_index_in_dim(parts, (member + shift) % count, 0, keepdims=False)
        got.append(lax.ppermute(send, axes, route))
    return jnp.stack(got)


def group_sum(value, axes, count, wire=None):
    sent = value if wire is None else value.astype(wire)
    total = sent.astype(value.dtype)
    for shift in range(1, count):
        route = [(source, (source + shift) % count) for source in range(count)]
        total = total + lax.ppermute(sent, axes, route).astype(value.dtype)
    return total


def body(activations, out_grad, gate_weights, routes, momentum):
    expert_count = lax.axis_size("expert")
    zlo_count = lax.axis_size("zlo")
    zhi_count = lax.axis_size("zhi")
    z_count = zhi_count * zlo_count
    tokens_here, slots_token, hidden_width = activations.shape
    model_width = out_grad.shape[1]
    own_rows = momentum.shape[0]
    expert_total = EXP_DEV * expert_count
    group_size = zlo_count * 2
    group = ("zlo", "core")

    grad_parts = out_grad.reshape(tokens_here, group_size, own_rows).transpose(1, 0, 2)
    grad_mine = group_exchange(grad_parts, group, group_size)
    grad_mine, activations = lax.optimization_barrier((grad_mine, activations))
    grad_all = lax.all_gather(grad_mine, ("zhi", "expert"), axis=1, tiled=False)
    grad_all = grad_all.reshape(-1, own_rows)

    numbers = jnp.arange(expert_total, dtype=jnp.int32)
    matched = routes[:, :, None] == numbers[None, None, :]
    flat_hidden = activations.reshape(tokens_here * slots_token, hidden_width)
    eye = (
        jnp.arange(tokens_here, dtype=jnp.int32)[:, None, None]
        == jnp.arange(tokens_here, dtype=jnp.int32)[None, :, None]
    )
    selector = (matched.transpose(2, 0, 1)[:, :, None, :] & eye[None]).astype(jnp.bfloat16)
    selector = selector.reshape(expert_total * tokens_here, tokens_here * slots_token)
    chosen = jnp.dot(selector, flat_hidden, preferred_element_type=jnp.float32)
    scale = jnp.sum(jnp.where(matched, gate_weights[:, :, None], 0.0), axis=1)
    scale = scale.T.reshape(expert_total * tokens_here, 1)
    scaled_hidden = (scale * chosen).astype(jnp.bfloat16)
    scaled_hidden = scaled_hidden.reshape(expert_count, EXP_DEV, tokens_here, hidden_width)
    scaled_hidden = scaled_hidden.transpose(1, 0, 2, 3).reshape(expert_total, tokens_here, hidden_width)
    got_hidden = lax.all_to_all(
        scaled_hidden, ("zhi", "expert"), split_axis=0, concat_axis=0, tiled=True
    )
    got_hidden = group_gather(got_hidden, group, group_size)
    got_hidden = got_hidden.reshape(-1, hidden_width)

    grad_all, got_hidden = lax.optimization_barrier((grad_all, got_hidden))
    gradient = lax.dot_general(
        grad_all, got_hidden, (((0,), (0,)), ((), ())), preferred_element_type=jnp.float32
    )
    gradient = lax.optimization_barrier(gradient)

    new_momentum = MOMENT * momentum + gradient
    ahead = gradient + MOMENT * new_momentum
    square_sum = group_sum(jnp.sum(ahead * ahead), group, group_size)
    raw_gram = group_sum(gram_of(ahead.astype(jnp.bfloat16)), group, group_size, jnp.bfloat16)
    norm_value = jnp.sqrt(square_sum)
    scaled = (ahead / (norm_value + EPSILON)).astype(jnp.bfloat16)
    scaled = lax.optimization_barrier(scaled)
    inverse = 1.0 / (norm_value + EPSILON)
    for turn_index in range(NS_ITERS):
        if turn_index == 0:
            gram = (raw_gram * (inverse * inverse)).astype(jnp.bfloat16)
        else:
            gram = group_sum(gram_of(scaled), group, group_size, jnp.bfloat16).astype(jnp.bfloat16)
        scaled = newton_update(scaled, gram)
    update = (math.sqrt(model_width) * scaled.astype(jnp.float32)).astype(jnp.bfloat16)
    return (update, new_momentum)


def solution(mesh):
    dp_count = mesh.shape["dp"]
    expert_count = mesh.shape["expert"]
    group_size = dp_count // EXP_DEV
    zlo = group_size // 2
    zhi = dp_count // 2 // zlo
    devices = np.asarray(mesh.devices).reshape(zhi, zlo, 2, expert_count)
    fine = Mesh(devices, ("zhi", "zlo", "core", "expert"))
    rows = ("zhi", "zlo", "core", "expert")
    cols = ("expert", "zhi", "zlo", "core")
    in_specs = (
        P(rows, None, None),
        P(rows, None),
        P(rows, None),
        P(rows, None),
        P(cols, None),
    )
    out_specs = (P(cols, None), P(cols, None))
    return jax.shard_map(body, mesh=fine, in_specs=in_specs, out_specs=out_specs, check_vma=False)
```
